32 devices in a mesh: outer: 8 (over z, y), inner: 4 (over x, core).
Axes of the slice: x: 2, y: 2, z: 4, core: 2. Of those that a mesh axis runs over, the one named last changes fastest.
Arguments:
- query: bfloat16 [4096, 2048], P(('outer', 'inner')), may hold values from -6 to 6
- key_in: bfloat16 [4096, 2048], P(('outer', 'inner')), may hold values from -6 to 6
- value_in: bfloat16 [4096, 2048], P(('outer', 'inner')), may hold values from -6 to 6
- filters: bfloat16 [4096, 128], P(('outer', 'inner')), may hold values from -1 to 1
- group_index: int32 [2048], replicated, may hold values from 0 to 127
- skip_gain: float32 [2048], replicated, may hold values from -1 to 1
Outputs:
- hyena_out: bfloat16 [4096, 2048], P(('outer', 'inner'))
The draws below stay inside these ranges and needn't reach their ends.
All inputs are finite; a program needn't handle non-finite values.
Results may differ from the reference program's by a relative error of at most 0.005.
Values may be sent and summed in bfloat16 or wider, within the bound.
No kernel may reach another device: no remote copies, remote signals or barrier semaphores. Data moves between devices by JAX's collectives and lax.ppermute only.
A program may use at most 64 MiB of HBM per device.

```python
import math
import jax
import jax.numpy as jnp
from jax import lax

CHANNELS = 2048
GROUPS = 128
SEQ = 4096


def rough_rows(key):
    return jax.random.truncated_normal(key, -2.5, 2.5, (SEQ, CHANNELS), jnp.float32)


def level_rows(log_start, log_end):
    fraction = jnp.arange(SEQ, dtype=jnp.float32)[:, None] / float(SEQ)
    return jnp.exp(log_start + (log_end - log_start) * fraction)


def draw_key_in(key, part):
    values = rough_rows(jax.random.fold_in(key, 21))
    falling = level_rows(0.25 * math.log(30.0), -0.25 * math.log(30.0))
    return (values * falling).astype(jnp.bfloat16)


def draw_value_in(key, part):
    values = rough_rows(jax.random.fold_in(key, 22))
    falling = level_rows(0.25 * math.log(30.0), -0.25 * math.log(30.0))
    return (values * falling).astype(jnp.bfloat16)


def draw_query(key, part):
    values = rough_rows(jax.random.fold_in(key, 23))
    rising = level_rows(math.log(2.35) - math.log(30.0), math.log(2.35))
    return (values * rising).astype(jnp.bfloat16)


def draw_filters(key, part):
    key_rough = jax.random.fold_in(key, 11)
    key_slow = jax.random.fold_in(key, 12)
    key_rate = jax.random.fold_in(key, 13)
    key_kind = jax.random.fold_in(key, 14)
    length = float(SEQ)
    slow_draw = jax.random.uniform(key_slow, (GROUPS,), jnp.float32)
    rate_draw = jax.random.uniform(key_rate, (GROUPS,), jnp.float32)
    kind_draw = jax.random.uniform(key_kind, (GROUPS,), jnp.float32)
    slow_lo = math.log(0.3 / length)
    slow_hi = math.log(2.3 / length)
    fast_hi = math.log(1.0 / 30.0)
    middle_hi = min(math.log(30.0 / length), fast_hi)
    slow_share = 0.5
    is_slow = slow_draw < slow_share
    is_middle = kind_draw < 0.5
    other_rate = jnp.where(is_middle, slow_hi + rate_draw * (middle_hi - slow_hi), middle_hi + rate_draw * (fast_hi - middle_hi))
    log_rate = jnp.where(is_slow, slow_lo + rate_draw * (slow_hi - slow_lo), other_rate)
    rates = jnp.exp(log_rate)
    positions = jnp.arange(SEQ, dtype=jnp.float32)[:, None]
    envelope = jnp.sqrt(2.0 * rates)[None, :] * jnp.exp(-rates[None, :] * positions)
    rough_part = jax.random.truncated_normal(key_rough, -4.0, 4.0, (SEQ, GROUPS), jnp.float32)
    values = rough_part * envelope
    return jnp.clip(values, -1.0, 1.0).astype(jnp.bfloat16)


def with_ends(drawn, key, smallest, top_value):
    longest = drawn.shape.index(max(drawn.shape))
    spots = []
    for shift in (0, 1):
        where = [jax.random.randint(jax.random.fold_in(key, axis), (), 0, length) for axis, length in enumerate(drawn.shape)]
        where[longest] = (where[longest] + shift) % drawn.shape[longest]
        spots.append(tuple(where))
    return drawn.at[spots[0]].set(smallest).at[spots[1]].set(top_value)


def setup_inputs(seed: int = 0) -> dict:
    splits = jax.random.split(jax.random.key(seed), 7)
    query = draw_query(jax.random.fold_in(splits[6], 71), 0)
    key_in = draw_key_in(jax.random.fold_in(splits[6], 71), 0)
    value_in = draw_value_in(jax.random.fold_in(splits[6], 71), 0)
    filters = draw_filters(jax.random.fold_in(splits[6], 71), 0)
    group_index = with_ends(jax.random.randint(splits[4], (CHANNELS,), 0, GROUPS), jax.random.fold_in(splits[4], 1), 0, GROUPS - 1).astype(jnp.int32)
    skip_gain = jnp.clip(jax.random.uniform(splits[5], (CHANNELS,), jnp.float32, -1.0, 1.0), -1.0, 1.0)
    return {"query": query, "key_in": key_in, "value_in": value_in, "filters": filters, "group_index": group_index, "skip_gain": skip_gain}


def reference(query, key_in, value_in, filters, group_index, skip_gain):
    mixed = (key_in.astype(jnp.float32) * value_in.astype(jnp.float32)).astype(jnp.bfloat16)
    mixed_wide = mixed.astype(jnp.float32)
    filters_wide = filters.astype(jnp.float32)
    length = mixed.shape[0]
    channels = mixed.shape[1]
    blocksize = min(channels, 256)
    nblocks = channels // blocksize
    fft_len = 2 * length
    filter_spectrum = jnp.fft.rfft(filters_wide, n=fft_len, axis=0)
    blocks_data = mixed_wide.reshape(length, nblocks, blocksize).transpose(1, 0, 2)
    blocks_group = group_index.reshape(nblocks, blocksize)

    def convolve(block_pair):
        columns, groups_here = block_pair
        spectrum = jnp.fft.rfft(columns, n=fft_len, axis=0)
        return jnp.fft.irfft(spectrum * filter_spectrum[:, groups_here], n=fft_len, axis=0)[:length]

    convolved = lax.map(convolve, (blocks_data, blocks_group))
    convolved = convolved.transpose(1, 0, 2).reshape(length, channels)
    return (query.astype(jnp.float32) * (convolved + skip_gain[None, :] * mixed_wide)).astype(jnp.bfloat16)
```

```python
import math

import jax
import jax.numpy as jnp
from jax import lax
from jax.sharding import PartitionSpec as P


def contract(pattern, left_op, right_op):
    return jnp.einsum(
        pattern,
        left_op,
        right_op,
        precision=lax.Precision.HIGH,
        preferred_element_type=jnp.float32,
    )


def angles_of(numerator, period):
    return 2.0 * math.pi / period * jnp.mod(numerator, period).astype(jnp.float32)


def dft_table(count_out, count_in, period):
    index_grid = (
        jnp.arange(count_out, dtype=jnp.int32)[:, None]
        * jnp.arange(count_in, dtype=jnp.int32)[None, :]
    )
    phases = angles_of(index_grid, period)
    return (jnp.cos(phases), jnp.sin(phases))


def rotate(real_part, imag_part, phases, direction):
    cosine = jnp.cos(phases)
    sine_part = jnp.sin(phases)
    if direction < 0:
        return (
            real_part * cosine + imag_part * sine_part,
            imag_part * cosine - real_part * sine_part,
        )
    return (real_part * cosine - imag_part * sine_part, imag_part * cosine + real_part * sine_part)


def transform(pattern, table_cos, table_sin, real_part, imag_part, direction):
    out_real = contract(pattern, table_cos, real_part) - direction * contract(
        pattern, table_sin, imag_part
    )
    out_imag = contract(pattern, table_cos, imag_part) + direction * contract(
        pattern, table_sin, real_part
    )
    return (out_real, out_imag)


def by_channels(mixed, filters, group_index):
    n_dev = lax.axis_size("outer") * lax.axis_size("inner")
    row_count = mixed.shape[0]
    channels = mixed.shape[1]
    own_width = channels // n_dev
    size_a = 2 * n_dev
    padded = size_a * row_count
    chan_filters = jnp.take(filters, group_index, axis=1)
    sent = jnp.stack([mixed, chan_filters], axis=1).reshape(row_count, 2, n_dev, own_width)
    sent = sent.transpose(2, 0, 1, 3)
    got = lax.all_to_all(sent, ("outer", "inner"), split_axis=0, concat_axis=0, tiled=True)
    stacked = got.reshape(n_dev, row_count, 2 * own_width).astype(jnp.float32)
    first_cos, first_sin = dft_table(size_a, n_dev, size_a)
    real_part = contract("kn,nbc->kbc", first_cos, stacked)
    imag_part = -contract("kn,nbc->kbc", first_sin, stacked)
    twiddle = angles_of(
        jnp.arange(size_a, dtype=jnp.int32)[:, None]
        * jnp.arange(row_count, dtype=jnp.int32)[None, :],
        padded,
    )[:, :, None]
    real_part, imag_part = rotate(real_part, imag_part, twiddle, -1)
    second_cos, second_sin = dft_table(row_count, row_count, row_count)
    real_part, imag_part = transform(
        "qb,kbc->kqc", second_cos, second_sin, real_part, imag_part, -1
    )
    data_real = real_part[:, :, :own_width]
    data_imag = imag_part[:, :, :own_width]
    filter_real = real_part[:, :, own_width:]
    filter_imag = imag_part[:, :, own_width:]
    spec_real = data_real * filter_real - data_imag * filter_imag
    spec_imag = data_real * filter_imag + data_imag * filter_real
    real_part, imag_part = transform("bq,kqc->kbc", second_cos, second_sin, spec_real, spec_imag, 1)
    real_part, imag_part = rotate(real_part, imag_part, twiddle, 1)
    back_cos, back_sin = dft_table(n_dev, size_a, size_a)
    outcome = contract("nk,kbc->nbc", back_cos, real_part) - contract(
        "nk,kbc->nbc", back_sin, imag_part
    )
    outcome = (outcome * (1.0 / padded)).astype(jnp.bfloat16)
    returned = lax.all_to_all(outcome, ("outer", "inner"), split_axis=0, concat_axis=0, tiled=True)
    return returned.transpose(1, 0, 2).reshape(row_count, channels)


def on_device(query, key_in, value_in, filters, group_index, skip_gain):
    mixed = (key_in.astype(jnp.float32) * value_in.astype(jnp.float32)).astype(jnp.bfloat16)
    convolved = by_channels(mixed, filters, group_index)
    mixed_wide = mixed.astype(jnp.float32)
    return (query.astype(jnp.float32) * (convolved + skip_gain[None, :] * mixed_wide)).astype(
        jnp.bfloat16
    )


def solution(mesh):
    placed = (
        P(("outer", "inner"), None),
        P(("outer", "inner"), None),
        P(("outer", "inner"), None),
        P(("outer", "inner"), None),
        P(),
        P(),
    )
    return jax.shard_map(
        on_device,
        mesh=mesh,
        in_specs=placed,
        out_specs=P(("outer", "inner"), None),
        check_vma=False,
    )
```

```python
import math

import jax
import jax.numpy as jnp
from jax import lax
from jax.sharding import PartitionSpec as P


def contract(pattern, left_op, right_op):
    return jnp.einsum(
        pattern,
        left_op,
        right_op,
        precision=lax.Precision.HIGH,
        preferred_element_type=jnp.float32,
    )


def angles_of(numerator, period):
    return 2.0 * math.pi / period * jnp.mod(numerator, period).astype(jnp.float32)


def dft_table(count_out, count_in, period):
    index_grid = (
        jnp.arange(count_out, dtype=jnp.int32)[:, None]
        * jnp.arange(count_in, dtype=jnp.int32)[None, :]
    )
    phases = angles_of(index_grid, period)
    return (jnp.cos(phases), jnp.sin(phases))


def rotate(real_part, imag_part, phases, direction):
    cosine = jnp.cos(phases)
    sine_part = jnp.sin(phases)
    if direction < 0:
        return (
            real_part * cosine + imag_part * sine_part,
            imag_part * cosine - real_part * sine_part,
        )
    return (real_part * cosine - imag_part * sine_part, imag_part * cosine + real_part * sine_part)


def transform(pattern, table_cos, table_sin, real_part, imag_part, direction):
    out_real = contract(pattern, table_cos, real_part) - direction * contract(
        pattern, table_sin, imag_part
    )
    out_imag = contract(pattern, table_cos, imag_part) + direction * contract(
        pattern, table_sin, real_part
    )
    return (out_real, out_imag)


def by_channels(mixed, filters, group_index):
    n_dev = lax.axis_size("outer") * lax.axis_size("inner")
    row_count = mixed.shape[0]
    channels = mixed.shape[1]
    own_width = channels // n_dev
    size_a = 2 * n_dev
    padded = size_a * row_count
    chan_filters = jnp.take(filters, group_index, axis=1)
    sent = jnp.stack([mixed, chan_filters], axis=1).reshape(row_count, 2, n_dev, own_width)
    sent = sent.transpose(2, 0, 1, 3)
    got = lax.all_to_all(sent, ("outer", "inner"), split_axis=0, concat_axis=0, tiled=True)
    stacked = got.reshape(n_dev, row_count, 2 * own_width).astype(jnp.float32)
    first_cos, first_sin = dft_table(size_a, n_dev, size_a)
    first = contract("kn,nbc->kbc", jnp.concatenate([first_cos, -first_sin], axis=0), stacked)
    real_part = first[:size_a]
    imag_part = first[size_a:]
    twiddle = angles_of(
        jnp.arange(size_a, dtype=jnp.int32)[:, None]
        * jnp.arange(row_count, dtype=jnp.int32)[None, :],
        padded,
    )[:, :, None]
    real_part, imag_part = rotate(real_part, imag_part, twiddle, -1)
    second_cos, second_sin = dft_table(row_count, row_count, row_count)
    wide_cos = jnp.broadcast_to(second_cos[None], (size_a, row_count, row_count))
    wide_sin = jnp.broadcast_to(second_sin[None], (size_a, row_count, row_count))
    both = jnp.concatenate([real_part, imag_part], axis=2)
    by_cos = contract("kqb,kbc->kqc", wide_cos, both)
    by_sin = contract("kqb,kbc->kqc", wide_sin, both)
    width = 2 * own_width
    real_part = by_cos[:, :, :width] + by_sin[:, :, width:]
    imag_part = by_cos[:, :, width:] - by_sin[:, :, :width]
    data_real = real_part[:, :, :own_width]
    data_imag = imag_part[:, :, :own_width]
    filter_real = real_part[:, :, own_width:]
    filter_imag = imag_part[:, :, own_width:]
    spec_real = data_real * filter_real - data_imag * filter_imag
    spec_imag = data_real * filter_imag + data_imag * filter_real
    both = jnp.concatenate([spec_real, spec_imag], axis=2)
    by_cos = contract("kbq,kqc->kbc", wide_cos, both)
    by_sin = contract("kbq,kqc->kbc", wide_sin, both)
    real_part = by_cos[:, :, :own_width] - by_sin[:, :, own_width:]
    imag_part = by_cos[:, :, own_width:] + by_sin[:, :, :own_width]
    real_part, imag_part = rotate(real_part, imag_part, twiddle, 1)
    back_cos, back_sin = dft_table(n_dev, size_a, size_a)
    outcome = contract(
        "nk,kbc->nbc",
        jnp.concatenate([back_cos, -back_sin], axis=1),
        jnp.concatenate([real_part, imag_part], axis=0),
    )
    outcome = (outcome * (1.0 / padded)).astype(jnp.bfloat16)
    returned = lax.all_to_all(outcome, ("outer", "inner"), split_axis=0, concat_axis=0, tiled=True)
    return returned.transpose(1, 0, 2).reshape(row_count, channels)


def on_device(query, key_in, value_in, filters, group_index, skip_gain):
    mixed = (key_in.astype(jnp.float32) * value_in.astype(jnp.float32)).astype(jnp.bfloat16)
    convolved = by_channels(mixed, filters, group_index)
    mixed_wide = mixed.astype(jnp.float32)
    return (query.astype(jnp.float32) * (convolved + skip_gain[None, :] * mixed_wide)).astype(
        jnp.bfloat16
    )


def solution(mesh):
    placed = (
        P(("outer", "inner"), None),
        P(("outer", "inner"), None),
        P(("outer", "inner"), None),
        P(("outer", "inner"), None),
        P(),
        P(),
    )
    return jax.shard_map(
        on_device,
        mesh=mesh,
        in_specs=placed,
        out_specs=P(("outer", "inner"), None),
        check_vma=False,
    )
```

```python
import math

import jax
import jax.numpy as jnp
from jax import lax
from jax.sharding import PartitionSpec as P


def contract(pattern, left_op, right_op):
    return jnp.einsum(
        pattern,
        left_op,
        right_op,
        precision=lax.Precision.HIGH,
        preferred_element_type=jnp.float32,
    )


def angles_of(numerator, period):
    return 2.0 * math.pi / period * jnp.mod(numerator, period).astype(jnp.float32)


def dft_table(count_out, count_in, period):
    index_grid = (
        jnp.arange(count_out, dtype=jnp.int32)[:, None]
        * jnp.arange(count_in, dtype=jnp.int32)[None, :]
    )
    phases = angles_of(index_grid, period)
    return (jnp.cos(phases), jnp.sin(phases))


def rotate(real_part, imag_part, phases, direction):
    cosine = jnp.cos(phases)
    sine_part = jnp.sin(phases)
    if direction < 0:
        return (
            real_part * cosine + imag_part * sine_part,
            imag_part * cosine - real_part * sine_part,
        )
    return (real_part * cosine - imag_part * sine_part, imag_part * cosine + real_part * sine_part)


def transform(pattern, table_cos, table_sin, real_part, imag_part, direction):
    out_real = contract(pattern, table_cos, real_part) - direction * contract(
        pattern, table_sin, imag_part
    )
    out_imag = contract(pattern, table_cos, imag_part) + direction * contract(
        pattern, table_sin, real_part
    )
    return (out_real, out_imag)


def by_channels(mixed, filters, group_index):
    n_dev = lax.axis_size("outer") * lax.axis_size("inner")
    row_count = mixed.shape[0]
    channels = mixed.shape[1]
    own_width = channels // n_dev
    size_a = 2 * n_dev
    padded = size_a * row_count
    chan_filters = jnp.take(filters.T, group_index, axis=0)
    sent = jnp.stack([mixed.T, chan_filters], axis=0).reshape(2, n_dev, own_width, row_count)
    sent = sent.transpose(1, 0, 2, 3)
    got = lax.all_to_all(sent, ("outer", "inner"), split_axis=0, concat_axis=0, tiled=True)
    stacked = got.reshape(n_dev, 2 * own_width, row_count).astype(jnp.float32)
    first_cos, first_sin = dft_table(size_a, n_dev, size_a)
    first = contract("kn,ncb->kcb", jnp.concatenate([first_cos, -first_sin], axis=0), stacked)
    twiddle = angles_of(
        jnp.arange(size_a, dtype=jnp.int32)[:, None]
        * jnp.arange(row_count, dtype=jnp.int32)[None, :],
        padded,
    )[:, None, :]
    real_part, imag_part = rotate(first[:size_a], first[size_a:], twiddle, -1)
    second_cos, second_sin = dft_table(row_count, row_count, row_count)
    table = jnp.concatenate([second_cos, second_sin], axis=1)
    prod = contract("kcb,bq->kcq", jnp.concatenate([real_part, imag_part], axis=0), table)
    real_part = prod[:size_a, :, :row_count] + prod[size_a:, :, row_count:]
    imag_part = prod[size_a:, :, :row_count] - prod[:size_a, :, row_count:]
    data_real = real_part[:, :own_width]
    data_imag = imag_part[:, :own_width]
    filter_real = real_part[:, own_width:]
    filter_imag = imag_part[:, own_width:]
    spec_real = data_real * filter_real - data_imag * filter_imag
    spec_imag = data_real * filter_imag + data_imag * filter_real
    prod = contract("kcq,qb->kcb", jnp.concatenate([spec_real, spec_imag], axis=0), table)
    real_part = prod[:size_a, :, :row_count] - prod[size_a:, :, row_count:]
    imag_part = prod[size_a:, :, :row_count] + prod[:size_a, :, row_count:]
    real_part, imag_part = rotate(real_part, imag_part, twiddle, 1)
    back_cos, back_sin = dft_table(n_dev, size_a, size_a)
    outcome = contract(
        "nk,kcb->ncb",
        jnp.concatenate([back_cos, -back_sin], axis=1),
        jnp.concatenate([real_part, imag_part], axis=0),
    )
    outcome = (outcome * (1.0 / padded)).astype(jnp.bfloat16)
    returned = lax.all_to_all(outcome, ("outer", "inner"), split_axis=0, concat_axis=0, tiled=True)
    return returned.reshape(channels, row_count).T


def on_device(query, key_in, value_in, filters, group_index, skip_gain):
    mixed = (key_in.astype(jnp.float32) * value_in.astype(jnp.float32)).astype(jnp.bfloat16)
    convolved = by_channels(mixed, filters, group_index)
    mixed_wide = mixed.astype(jnp.float32)
    return (query.astype(jnp.float32) * (convolved + skip_gain[None, :] * mixed_wide)).astype(
        jnp.bfloat16
    )


def solution(mesh):
    placed = (
        P(("outer", "inner"), None),
        P(("outer", "inner"), None),
        P(("outer", "inner"), None),
        P(("outer", "inner"), None),
        P(),
        P(),
    )
    return jax.shard_map(
        on_device,
        mesh=mesh,
        in_specs=placed,
        out_specs=P(("outer", "inner"), None),
        check_vma=False,
    )
```

```python
import math

import jax
import jax.numpy as jnp
from jax import lax
from jax.sharding import PartitionSpec as P
from jax.experimental import pallas as pl


def contract(pattern, left_op, right_op):
    return jnp.einsum(
        pattern,
        left_op,
        right_op,
        precision=lax.Precision.HIGH,
        preferred_element_type=jnp.float32,
    )


def angles_of(numerator, period):
    return 2.0 * math.pi / period * jnp.mod(numerator, period).astype(jnp.float32)


def dft_table(count_out, count_in, period):
    index_grid = (
        jnp.arange(count_out, dtype=jnp.int32)[:, None]
        * jnp.arange(count_in, dtype=jnp.int32)[None, :]
    )
    phases = angles_of(index_grid, period)
    return (jnp.cos(phases), jnp.sin(phases))


def rotate(real_part, imag_part, phases, direction):
    cosine = jnp.cos(phases)
    sine_part = jnp.sin(phases)
    if direction < 0:
        return (
            real_part * cosine + imag_part * sine_part,
            imag_part * cosine - real_part * sine_part,
        )
    return (real_part * cosine - imag_part * sine_part, imag_part * cosine + real_part * sine_part)


def transform(pattern, table_cos, table_sin, real_part, imag_part, direction):
    out_real = contract(pattern, table_cos, real_part) - direction * contract(
        pattern, table_sin, imag_part
    )
    out_imag = contract(pattern, table_cos, imag_part) + direction * contract(
        pattern, table_sin, real_part
    )
    return (out_real, out_imag)


def select_kernel(index_ref, filters_ref, out_ref):
    index = index_ref[...]
    groups = filters_ref.shape[1]
    onehot = (
        index == lax.broadcasted_iota(jnp.int32, (index.shape[0], groups), 1)
    ).astype(jnp.bfloat16)
    out_ref[...] = lax.dot_general(
        onehot,
        filters_ref[...],
        (((1,), (1,)), ((), ())),
        preferred_element_type=jnp.float32,
    ).astype(out_ref.dtype)


def select_filters(filters, group_index):
    channels = group_index.shape[0]
    return pl.pallas_call(
        select_kernel,
        out_shape=jax.ShapeDtypeStruct((channels, filters.shape[0]), jnp.bfloat16),
    )(group_index.reshape(channels, 1), filters)


def complex_table(cos_part, sin_part, direction):
    return jnp.concatenate(
        [
            jnp.concatenate([cos_part, direction * sin_part], axis=1),
            jnp.concatenate([-direction * sin_part, cos_part], axis=1),
        ],
        axis=0,
    )


def by_channels(mixed, filters, group_index):
    n_dev = lax.axis_size("outer") * lax.axis_size("inner")
    row_count = mixed.shape[0]
    channels = mixed.shape[1]
    own_width = channels // n_dev
    size_a = 2 * n_dev
    padded = size_a * row_count
    chan_filters = select_filters(filters, group_index)
    sent = jnp.stack([mixed.T, chan_filters], axis=0).reshape(2, n_dev, own_width, row_count)
    sent = sent.transpose(1, 0, 2, 3)
    got = lax.all_to_all(sent, ("outer", "inner"), split_axis=0, concat_axis=0, tiled=True)
    stacked = got.reshape(n_dev, 2 * own_width, row_count).astype(jnp.float32)
    first_cos, first_sin = dft_table(size_a, n_dev, size_a)
    first = contract("kn,ncb->kcb", jnp.concatenate([first_cos, -first_sin], axis=0), stacked)
    twiddle = angles_of(
        jnp.arange(size_a, dtype=jnp.int32)[:, None]
        * jnp.arange(row_count, dtype=jnp.int32)[None, :],
        padded,
    )[:, None, :]
    real_part, imag_part = rotate(first[:size_a], first[size_a:], twiddle, -1)
    second_cos, second_sin = dft_table(row_count, row_count, row_count)
    prod = contract(
        "kcb,bq->kcq",
        jnp.concatenate([real_part, imag_part], axis=2),
        complex_table(second_cos, second_sin, -1),
    )
    data_real = prod[:, :own_width, :row_count]
    data_imag = prod[:, :own_width, row_count:]
    filter_real = prod[:, own_width:, :row_count]
    filter_imag = prod[:, own_width:, row_count:]
    spec_real = data_real * filter_real - data_imag * filter_imag
    spec_imag = data_real * filter_imag + data_imag * filter_real
    prod = contract(
        "kcq,qb->kcb",
        jnp.concatenate([spec_real, spec_imag], axis=2),
        complex_table(second_cos, second_sin, 1),
    )
    real_part, imag_part = rotate(prod[:, :, :row_count], prod[:, :, row_count:], twiddle, 1)
    back_cos, back_sin = dft_table(n_dev, size_a, size_a)
    outcome = contract(
        "nk,kcb->ncb",
        jnp.concatenate([back_cos, -back_sin], axis=1),
        jnp.concatenate([real_part, imag_part], axis=0),
    )
    outcome = (outcome * (1.0 / padded)).astype(jnp.bfloat16)
    returned = lax.all_to_all(outcome, ("outer", "inner"), split_axis=0, concat_axis=0, tiled=True)
    return returned.reshape(channels, row_count).T


def on_device(query, key_in, value_in, filters, group_index, skip_gain):
    mixed = (key_in.astype(jnp.float32) * value_in.astype(jnp.float32)).astype(jnp.bfloat16)
    convolved = by_channels(mixed, filters, group_index)
    mixed_wide = mixed.astype(jnp.float32)
    return (query.astype(jnp.float32) * (convolved + skip_gain[None, :] * mixed_wide)).astype(
        jnp.bfloat16
    )


def solution(mesh):
    placed = (
        P(("outer", "inner"), None),
        P(("outer", "inner"), None),
        P(("outer", "inner"), None),
        P(("outer", "inner"), None),
        P(),
        P(),
    )
    return jax.shard_map(
        on_device,
        mesh=mesh,
        in_specs=placed,
        out_specs=P(("outer", "inner"), None),
        check_vma=False,
    )
```

```python
import math

import jax
import jax.numpy as jnp
from jax import lax
from jax.sharding import PartitionSpec as P
from jax.experimental import pallas as pl


def contract(pattern, left_op, right_op):
    return jnp.einsum(
        pattern,
        left_op,
        right_op,
        precision=lax.Precision.HIGH,
        preferred_element_type=jnp.float32,
    )


def angles_of(numerator, period):
    return 2.0 * math.pi / period * jnp.mod(numerator, period).astype(jnp.float32)


def dft_table(count_out, count_in, period):
    index_grid = (
        jnp.arange(count_out, dtype=jnp.int32)[:, None]
        * jnp.arange(count_in, dtype=jnp.int32)[None, :]
    )
    phases = angles_of(index_grid, period)
    return (jnp.cos(phases), jnp.sin(phases))


def rotate(real_part, imag_part, phases, direction):
    cosine = jnp.cos(phases)
    sine_part = jnp.sin(phases)
    if direction < 0:
        return (
            real_part * cosine + imag_part * sine_part,
            imag_part * cosine - real_part * sine_part,
        )
    return (real_part * cosine - imag_part * sine_part, imag_part * cosine + real_part * sine_part)


def transform(pattern, table_cos, table_sin, real_part, imag_part, direction):
    out_real = contract(pattern, table_cos, real_part) - direction * contract(
        pattern, table_sin, imag_part
    )
    out_imag = contract(pattern, table_cos, imag_part) + direction * contract(
        pattern, table_sin, real_part
    )
    return (out_real, out_imag)


def select_kernel(index_ref, filters_ref, out_ref):
    index = index_ref[...]
    groups = filters_ref.shape[1]
    block = out_ref.shape[2]
    onehot = (
        index == lax.broadcasted_iota(jnp.int32, (index.shape[0], groups), 1)
    ).astype(jnp.bfloat16)
    picked = lax.dot_general(
        onehot,
        filters_ref[...],
        (((1,), (1,)), ((), ())),
        preferred_element_type=jnp.float32,
    )
    for n in range(out_ref.shape[0]):
        out_ref[n] = picked[:, n * block : (n + 1) * block].astype(out_ref.dtype)


def select_filters(filters, own_index, n_blocks, block):
    width = own_index.shape[0]
    return pl.pallas_call(
        select_kernel,
        out_shape=jax.ShapeDtypeStruct((n_blocks, width, block), jnp.bfloat16),
    )(own_index.reshape(width, 1), filters)


def complex_table(cos_part, sin_part, direction):
    return jnp.concatenate(
        [
            jnp.concatenate([cos_part, direction * sin_part], axis=1),
            jnp.concatenate([-direction * sin_part, cos_part], axis=1),
        ],
        axis=0,
    )


def by_channels(mixed, filters, group_index):
    n_dev = lax.axis_size("outer") * lax.axis_size("inner")
    row_count = mixed.shape[0]
    channels = mixed.shape[1]
    own_width = channels // n_dev
    size_a = 2 * n_dev
    padded = size_a * row_count
    all_filters = lax.all_gather(filters, ("outer", "inner"), axis=0, tiled=True)
    me = lax.axis_index("outer") * lax.axis_size("inner") + lax.axis_index("inner")
    own_index = lax.dynamic_slice(group_index, (me * own_width,), (own_width,))
    sent = mixed.T.reshape(n_dev, own_width, row_count)
    got = lax.all_to_all(sent, ("outer", "inner"), split_axis=0, concat_axis=0, tiled=True)
    chan_filters = select_filters(all_filters, own_index, n_dev, row_count)
    stacked = jnp.concatenate([got, chan_filters], axis=1).astype(jnp.float32)
    first_cos, first_sin = dft_table(size_a, n_dev, size_a)
    first = contract("kn,ncb->kcb", jnp.concatenate([first_cos, -first_sin], axis=0), stacked)
    twiddle = angles_of(
        jnp.arange(size_a, dtype=jnp.int32)[:, None]
        * jnp.arange(row_count, dtype=jnp.int32)[None, :],
        padded,
    )[:, None, :]
    real_part, imag_part = rotate(first[:size_a], first[size_a:], twiddle, -1)
    second_cos, second_sin = dft_table(row_count, row_count, row_count)
    prod = contract(
        "kcb,bq->kcq",
        jnp.concatenate([real_part, imag_part], axis=2),
        complex_table(second_cos, second_sin, -1),
    )
    data_real = prod[:, :own_width, :row_count]
    data_imag = prod[:, :own_width, row_count:]
    filter_real = prod[:, own_width:, :row_count]
    filter_imag = prod[:, own_width:, row_count:]
    spec_real = data_real * filter_real - data_imag * filter_imag
    spec_imag = data_real * filter_imag + data_imag * filter_real
    prod = contract(
        "kcq,qb->kcb",
        jnp.concatenate([spec_real, spec_imag], axis=2),
        complex_table(second_cos, second_sin, 1),
    )
    real_part, imag_part = rotate(prod[:, :, :row_count], prod[:, :, row_count:], twiddle, 1)
    back_cos, back_sin = dft_table(n_dev, size_a, size_a)
    outcome = contract(
        "nk,kcb->ncb",
        jnp.concatenate([back_cos, -back_sin], axis=1),
        jnp.concatenate([real_part, imag_part], axis=0),
    )
    outcome = (outcome * (1.0 / padded)).astype(jnp.bfloat16)
    returned = lax.all_to_all(outcome, ("outer", "inner"), split_axis=0, concat_axis=0, tiled=True)
    return returned.reshape(channels, row_count).T


def on_device(query, key_in, value_in, filters, group_index, skip_gain):
    mixed = (key_in.astype(jnp.float32) * value_in.astype(jnp.float32)).astype(jnp.bfloat16)
    convolved = by_channels(mixed, filters, group_index)
    mixed_wide = mixed.astype(jnp.float32)
    return (query.astype(jnp.float32) * (convolved + skip_gain[None, :] * mixed_wide)).astype(
        jnp.bfloat16
    )


def solution(mesh):
    placed = (
        P(("outer", "inner"), None),
        P(("outer", "inner"), None),
        P(("outer", "inner"), None),
        P(("outer", "inner"), None),
        P(),
        P(),
    )
    return jax.shard_map(
        on_device,
        mesh=mesh,
        in_specs=placed,
        out_specs=P(("outer", "inner"), None),
        check_vma=False,
    )
```

```python
import math

import jax
import jax.numpy as jnp
from jax import lax
from jax.sharding import PartitionSpec as P
from jax.experimental import pallas as pl


def contract(pattern, left_op, right_op):
    return jnp.einsum(
        pattern,
        left_op,
        right_op,
        precision=lax.Precision.HIGH,
        preferred_element_type=jnp.float32,
    )


def angles_of(numerator, period):
    return 2.0 * math.pi / period * jnp.mod(numerator, period).astype(jnp.float32)


def dft_table(count_out, count_in, period):
    index_grid = (
        jnp.arange(count_out, dtype=jnp.int32)[:, None]
        * jnp.arange(count_in, dtype=jnp.int32)[None, :]
    )
    phases = angles_of(index_grid, period)
    return (jnp.cos(phases), jnp.sin(phases))


def rotate(real_part, imag_part, phases, direction):
    cosine = jnp.cos(phases)
    sine_part = jnp.sin(phases)
    if direction < 0:
        return (
            real_part * cosine + imag_part * sine_part,
            imag_part * cosine - real_part * sine_part,
        )
    return (real_part * cosine - imag_part * sine_part, imag_part * cosine + real_part * sine_part)


def transform(pattern, table_cos, table_sin, real_part, imag_part, direction):
    out_real = contract(pattern, table_cos, real_part) - direction * contract(
        pattern, table_sin, imag_part
    )
    out_imag = contract(pattern, table_cos, imag_part) + direction * contract(
        pattern, table_sin, real_part
    )
    return (out_real, out_imag)


def select_kernel(index_ref, filters_ref, out_ref):
    index = index_ref[...]
    groups = filters_ref.shape[1]
    onehot = (
        index == lax.broadcasted_iota(jnp.int32, (index.shape[0], groups), 1)
    ).astype(jnp.bfloat16)
    out_ref[...] = lax.dot_general(
        onehot,
        filters_ref[...],
        (((1,), (1,)), ((), ())),
        preferred_element_type=jnp.float32,
    ).astype(out_ref.dtype)


def select_filters(filters, group_index):
    channels = group_index.shape[0]
    return pl.pallas_call(
        select_kernel,
        out_shape=jax.ShapeDtypeStruct((channels, filters.shape[0]), jnp.bfloat16),
    )(group_index.reshape(channels, 1), filters)


def complex_table(cos_part, sin_part, direction):
    return jnp.concatenate(
        [
            jnp.concatenate([cos_part, direction * sin_part], axis=1),
            jnp.concatenate([-direction * sin_part, cos_part], axis=1),
        ],
        axis=0,
    )


def convolve_block(got, n_dev, row_count):
    own_width = got.shape[2]
    size_a = 2 * n_dev
    padded = size_a * row_count
    stacked = got.reshape(n_dev, 2 * own_width, row_count).astype(jnp.float32)
    first_cos, first_sin = dft_table(size_a, n_dev, size_a)
    first = contract("kn,ncb->kcb", jnp.concatenate([first_cos, -first_sin], axis=0), stacked)
    twiddle = angles_of(
        jnp.arange(size_a, dtype=jnp.int32)[:, None]
        * jnp.arange(row_count, dtype=jnp.int32)[None, :],
        padded,
    )[:, None, :]
    real_part, imag_part = rotate(first[:size_a], first[size_a:], twiddle, -1)
    second_cos, second_sin = dft_table(row_count, row_count, row_count)
    prod = contract(
        "kcb,bq->kcq",
        jnp.concatenate([real_part, imag_part], axis=2),
        complex_table(second_cos, second_sin, -1),
    )
    data_real = prod[:, :own_width, :row_count]
    data_imag = prod[:, :own_width, row_count:]
    filter_real = prod[:, own_width:, :row_count]
    filter_imag = prod[:, own_width:, row_count:]
    spec_real = data_real * filter_real - data_imag * filter_imag
    spec_imag = data_real * filter_imag + data_imag * filter_real
    prod = contract(
        "kcq,qb->kcb",
        jnp.concatenate([spec_real, spec_imag], axis=2),
        complex_table(second_cos, second_sin, 1),
    )
    real_part, imag_part = rotate(prod[:, :, :row_count], prod[:, :, row_count:], twiddle, 1)
    back_cos, back_sin = dft_table(n_dev, size_a, size_a)
    outcome = contract(
        "nk,kcb->ncb",
        jnp.concatenate([back_cos, -back_sin], axis=1),
        jnp.concatenate([real_part, imag_part], axis=0),
    )
    return (outcome * (1.0 / padded)).astype(jnp.bfloat16)


def by_channels(mixed, filters, group_index):
    n_dev = lax.axis_size("outer") * lax.axis_size("inner")
    row_count = mixed.shape[0]
    channels = mixed.shape[1]
    own_width = channels // n_dev
    pieces = 2 if own_width % 16 == 0 else 1
    piece_width = own_width // pieces
    chan_filters = select_filters(filters, group_index)
    sent = jnp.stack([mixed.T, chan_filters], axis=0).reshape(
        2, n_dev, pieces, piece_width, row_count
    )
    sent = sent.transpose(2, 1, 0, 3, 4)
    arrived = [
        lax.all_to_all(sent[piece], ("outer", "inner"), split_axis=0, concat_axis=0, tiled=True)
        for piece in range(pieces)
    ]
    results = []
    outcome = None
    for piece in range(pieces):
        got = arrived[piece]
        if outcome is not None:
            outcome, got = lax.optimization_barrier((outcome, got))
        outcome = convolve_block(got, n_dev, row_count)
        results.append(
            lax.all_to_all(outcome, ("outer", "inner"), split_axis=0, concat_axis=0, tiled=True)
        )
    returned = jnp.stack(results, axis=1)
    return returned.reshape(channels, row_count).T


def on_device(query, key_in, value_in, filters, group_index, skip_gain):
    mixed = (key_in.astype(jnp.float32) * value_in.astype(jnp.float32)).astype(jnp.bfloat16)
    convolved = by_channels(mixed, filters, group_index)
    mixed_wide = mixed.astype(jnp.float32)
    return (query.astype(jnp.float32) * (convolved + skip_gain[None, :] * mixed_wide)).astype(
        jnp.bfloat16
    )


def solution(mesh):
    placed = (
        P(("outer", "inner"), None),
        P(("outer", "inner"), None),
        P(("outer", "inner"), None),
        P(("outer", "inner"), None),
        P(),
        P(),
    )
    return jax.shard_map(
        on_device,
        mesh=mesh,
        in_specs=placed,
        out_specs=P(("outer", "inner"), None),
        check_vma=False,
    )
```

```python
import math

import jax
import jax.numpy as jnp
from jax import lax
from jax.sharding import PartitionSpec as P
from jax.experimental import pallas as pl


def contract(pattern, left_op, right_op):
    return jnp.einsum(
        pattern,
        left_op,
        right_op,
        precision=lax.Precision.HIGH,
        preferred_element_type=jnp.float32,
    )


def angles_of(numerator, period):
    return 2.0 * math.pi / period * jnp.mod(numerator, period).astype(jnp.float32)


def dft_table(count_out, count_in, period):
    index_grid = (
        jnp.arange(count_out, dtype=jnp.int32)[:, None]
        * jnp.arange(count_in, dtype=jnp.int32)[None, :]
    )
    phases = angles_of(index_grid, period)
    return (jnp.cos(phases), jnp.sin(phases))


def rotate(real_part, imag_part, phases, direction):
    cosine = jnp.cos(phases)
    sine_part = jnp.sin(phases)
    if direction < 0:
        return (
            real_part * cosine + imag_part * sine_part,
            imag_part * cosine - real_part * sine_part,
        )
    return (real_part * cosine - imag_part * sine_part, imag_part * cosine + real_part * sine_part)


def transform(pattern, table_cos, table_sin, real_part, imag_part, direction):
    out_real = contract(pattern, table_cos, real_part) - direction * contract(
        pattern, table_sin, imag_part
    )
    out_imag = contract(pattern, table_cos, imag_part) + direction * contract(
        pattern, table_sin, real_part
    )
    return (out_real, out_imag)


def select_kernel(index_ref, filters_ref, out_ref):
    index = index_ref[...]
    groups = filters_ref.shape[1]
    onehot = (
        index == lax.broadcasted_iota(jnp.int32, (index.shape[0], groups), 1)
    ).astype(jnp.bfloat16)
    out_ref[...] = lax.dot_general(
        onehot,
        filters_ref[...],
        (((1,), (1,)), ((), ())),
        preferred_element_type=jnp.float32,
    ).astype(out_ref.dtype)


def select_filters(filters, group_index):
    channels = group_index.shape[0]
    return pl.pallas_call(
        select_kernel,
        out_shape=jax.ShapeDtypeStruct((channels, filters.shape[0]), jnp.bfloat16),
    )(group_index.reshape(channels, 1), filters)


def complex_table(cos_part, sin_part, direction):
    return jnp.concatenate(
        [
            jnp.concatenate([cos_part, direction * sin_part], axis=1),
            jnp.concatenate([-direction * sin_part, cos_part], axis=1),
        ],
        axis=0,
    )


def convolve_block(got, n_dev, row_count):
    own_width = got.shape[2]
    size_a = 2 * n_dev
    padded = size_a * row_count
    stacked = got.reshape(n_dev, 2 * own_width, row_count).astype(jnp.float32)
    first_cos, first_sin = dft_table(size_a, n_dev, size_a)
    first = contract("kn,ncb->kcb", jnp.concatenate([first_cos, -first_sin], axis=0), stacked)
    twiddle = angles_of(
        jnp.arange(size_a, dtype=jnp.int32)[:, None]
        * jnp.arange(row_count, dtype=jnp.int32)[None, :],
        padded,
    )[:, None, :]
    real_part, imag_part = rotate(first[:size_a], first[size_a:], twiddle, -1)
    second_cos, second_sin = dft_table(row_count, row_count, row_count)
    prod = contract(
        "kcb,bq->kcq",
        jnp.concatenate([real_part, imag_part], axis=2),
        complex_table(second_cos, second_sin, -1),
    )
    data_real = prod[:, :own_width, :row_count]
    data_imag = prod[:, :own_width, row_count:]
    filter_real = prod[:, own_width:, :row_count]
    filter_imag = prod[:, own_width:, row_count:]
    spec_real = data_real * filter_real - data_imag * filter_imag
    spec_imag = data_real * filter_imag + data_imag * filter_real
    prod = contract(
        "kcq,qb->kcb",
        jnp.concatenate([spec_real, spec_imag], axis=2),
        complex_table(second_cos, second_sin, 1),
    )
    real_part, imag_part = rotate(prod[:, :, :row_count], prod[:, :, row_count:], twiddle, 1)
    back_cos, back_sin = dft_table(n_dev, size_a, size_a)
    outcome = contract(
        "nk,kcb->ncb",
        jnp.concatenate([back_cos, -back_sin], axis=1),
        jnp.concatenate([real_part, imag_part], axis=0),
    )
    return (outcome * (1.0 / padded)).astype(jnp.bfloat16)


def by_channels(mixed, filters, group_index):
    n_dev = lax.axis_size("outer") * lax.axis_size("inner")
    row_count = mixed.shape[0]
    channels = mixed.shape[1]
    own_width = channels // n_dev
    pieces = 2 if own_width % 16 == 0 else 1
    piece_width = own_width // pieces
    chan_filters = select_filters(filters, group_index)
    sent = jnp.stack([mixed.T, chan_filters], axis=0).reshape(
        2, n_dev, pieces, piece_width, row_count
    )
    sent = sent.transpose(2, 1, 0, 3, 4)
    arrived = [
        lax.all_to_all(sent[piece], ("outer", "inner"), split_axis=0, concat_axis=0, tiled=True)
        for piece in range(pieces)
    ]
    results = []
    outcome = None
    for piece in range(pieces):
        got = arrived[piece]
        if outcome is not None:
            outcome, got = lax.optimization_barrier((outcome, got))
        outcome = convolve_block(got, n_dev, row_count)
        results.append(outcome)
    returned = lax.all_to_all(
        jnp.stack(results, axis=1), ("outer", "inner"), split_axis=0, concat_axis=0, tiled=True
    )
    return returned.reshape(channels, row_count).T


def on_device(query, key_in, value_in, filters, group_index, skip_gain):
    mixed = (key_in.astype(jnp.float32) * value_in.astype(jnp.float32)).astype(jnp.bfloat16)
    convolved = by_channels(mixed, filters, group_index)
    mixed_wide = mixed.astype(jnp.float32)
    return (query.astype(jnp.float32) * (convolved + skip_gain[None, :] * mixed_wide)).astype(
        jnp.bfloat16
    )


def solution(mesh):
    placed = (
        P(("outer", "inner"), None),
        P(("outer", "inner"), None),
        P(("outer", "inner"), None),
        P(("outer", "inner"), None),
        P(),
        P(),
    )
    return jax.shard_map(
        on_device,
        mesh=mesh,
        in_specs=placed,
        out_specs=P(("outer", "inner"), None),
        check_vma=False,
    )
```

```python
import math

import jax
import jax.numpy as jnp
from jax import lax
from jax.sharding import PartitionSpec as P
from jax.experimental import pallas as pl


def contract(pattern, left_op, right_op):
    return jnp.einsum(
        pattern,
        left_op,
        right_op,
        precision=lax.Precision.HIGH,
        preferred_element_type=jnp.float32,
    )


def angles_of(numerator, period):
    return 2.0 * math.pi / period * jnp.mod(numerator, period).astype(jnp.float32)


def dft_table(count_out, count_in, period):
    index_grid = (
        jnp.arange(count_out, dtype=jnp.int32)[:, None]
        * jnp.arange(count_in, dtype=jnp.int32)[None, :]
    )
    phases = angles_of(index_grid, period)
    return (jnp.cos(phases), jnp.sin(phases))


def rotate(real_part, imag_part, phases, direction):
    cosine = jnp.cos(phases)
    sine_part = jnp.sin(phases)
    if direction < 0:
        return (
            real_part * cosine + imag_part * sine_part,
            imag_part * cosine - real_part * sine_part,
        )
    return (real_part * cosine - imag_part * sine_part, imag_part * cosine + real_part * sine_part)


def transform(pattern, table_cos, table_sin, real_part, imag_part, direction):
    out_real = contract(pattern, table_cos, real_part) - direction * contract(
        pattern, table_sin, imag_part
    )
    out_imag = contract(pattern, table_cos, imag_part) + direction * contract(
        pattern, table_sin, real_part
    )
    return (out_real, out_imag)


def select_kernel(index_ref, filters_ref, out_ref):
    index = index_ref[...]
    groups = filters_ref.shape[1]
    onehot = (
        index == lax.broadcasted_iota(jnp.int32, (index.shape[0], groups), 1)
    ).astype(jnp.bfloat16)
    out_ref[...] = lax.dot_general(
        onehot,
        filters_ref[...],
        (((1,), (1,)), ((), ())),
        preferred_element_type=jnp.float32,
    ).astype(out_ref.dtype)


def select_filters(filters, group_index):
    channels = group_index.shape[0]
    return pl.pallas_call(
        select_kernel,
        out_shape=jax.ShapeDtypeStruct((channels, filters.shape[0]), jnp.bfloat16),
    )(group_index.reshape(channels, 1), filters)


def prep_kernel(key_ref, value_ref, filters_ref, index_ref, out_ref):
    pieces, n_dev, _, piece_width, _ = out_ref.shape
    mixed = (key_ref[...].astype(jnp.float32) * value_ref[...].astype(jnp.float32)).astype(
        jnp.bfloat16
    )
    mixed_t = mixed.astype(jnp.float32).T
    groups = filters_ref.shape[1]
    channels = index_ref.shape[1]
    onehot_t = (
        lax.broadcasted_iota(jnp.int32, (groups, channels), 0) == index_ref[...]
    ).astype(jnp.float32)
    picked = jnp.dot(
        filters_ref[...].astype(jnp.float32), onehot_t, preferred_element_type=jnp.float32
    ).T
    for dest in range(n_dev):
        for piece in range(pieces):
            low = (dest * pieces + piece) * piece_width
            out_ref[piece, dest, 0] = mixed_t[low : low + piece_width].astype(out_ref.dtype)
            out_ref[piece, dest, 1] = picked[low : low + piece_width].astype(out_ref.dtype)


def prepare(key_in, value_in, filters, group_index, n_dev, pieces):
    row_count, channels = key_in.shape
    piece_width = channels // (n_dev * pieces)
    return pl.pallas_call(
        prep_kernel,
        out_shape=jax.ShapeDtypeStruct(
            (pieces, n_dev, 2, piece_width, row_count), jnp.bfloat16
        ),
    )(key_in, value_in, filters, group_index.reshape(1, channels))


def complex_table(cos_part, sin_part, direction):
    return jnp.concatenate(
        [
            jnp.concatenate([cos_part, direction * sin_part], axis=1),
            jnp.concatenate([-direction * sin_part, cos_part], axis=1),
        ],
        axis=0,
    )


def convolve_block(got, n_dev, row_count):
    own_width = got.shape[2]
    size_a = 2 * n_dev
    padded = size_a * row_count
    stacked = got.reshape(n_dev, 2 * own_width, row_count).astype(jnp.float32)
    first_cos, first_sin = dft_table(size_a, n_dev, size_a)
    first = contract("kn,ncb->kcb", jnp.concatenate([first_cos, -first_sin], axis=0), stacked)
    twiddle = angles_of(
        jnp.arange(size_a, dtype=jnp.int32)[:, None]
        * jnp.arange(row_count, dtype=jnp.int32)[None, :],
        padded,
    )[:, None, :]
    real_part, imag_part = rotate(first[:size_a], first[size_a:], twiddle, -1)
    second_cos, second_sin = dft_table(row_count, row_count, row_count)
    prod = contract(
        "kcb,bq->kcq",
        jnp.concatenate([real_part, imag_part], axis=2),
        complex_table(second_cos, second_sin, -1),
    )
    data_real = prod[:, :own_width, :row_count]
    data_imag = prod[:, :own_width, row_count:]
    filter_real = prod[:, own_width:, :row_count]
    filter_imag = prod[:, own_width:, row_count:]
    spec_real = data_real * filter_real - data_imag * filter_imag
    spec_imag = data_real * filter_imag + data_imag * filter_real
    prod = contract(
        "kcq,qb->kcb",
        jnp.concatenate([spec_real, spec_imag], axis=2),
        complex_table(second_cos, second_sin, 1),
    )
    real_part, imag_part = rotate(prod[:, :, :row_count], prod[:, :, row_count:], twiddle, 1)
    back_cos, back_sin = dft_table(n_dev, size_a, size_a)
    outcome = contract(
        "nk,kcb->ncb",
        jnp.concatenate([back_cos, -back_sin], axis=1),
        jnp.concatenate([real_part, imag_part], axis=0),
    )
    return (outcome * (1.0 / padded)).astype(jnp.bfloat16)


def by_channels(mixed, key_in, value_in, filters, group_index):
    n_dev = lax.axis_size("outer") * lax.axis_size("inner")
    row_count = mixed.shape[0]
    channels = mixed.shape[1]
    own_width = channels // n_dev
    pieces = 2 if own_width % 16 == 0 else 1
    piece_width = own_width // pieces
    if piece_width % 16 == 0:
        sent = prepare(key_in, value_in, filters, group_index, n_dev, pieces)
    else:
        chan_filters = select_filters(filters, group_index)
        sent = jnp.stack([mixed.T, chan_filters], axis=0).reshape(
            2, n_dev, pieces, piece_width, row_count
        )
        sent = sent.transpose(2, 1, 0, 3, 4)
    arrived = [
        lax.all_to_all(sent[piece], ("outer", "inner"), split_axis=0, concat_axis=0, tiled=True)
        for piece in range(pieces)
    ]
    results = []
    outcome = None
    for piece in range(pieces):
        got = arrived[piece]
        if outcome is not None:
            outcome, got = lax.optimization_barrier((outcome, got))
        outcome = convolve_block(got, n_dev, row_count)
        results.append(outcome)
    returned = lax.all_to_all(
        jnp.stack(results, axis=1), ("outer", "inner"), split_axis=0, concat_axis=0, tiled=True
    )
    return returned.reshape(channels, row_count).T


def on_device(query, key_in, value_in, filters, group_index, skip_gain):
    mixed = (key_in.astype(jnp.float32) * value_in.astype(jnp.float32)).astype(jnp.bfloat16)
    convolved = by_channels(mixed, key_in, value_in, filters, group_index)
    mixed_wide = mixed.astype(jnp.float32)
    return (query.astype(jnp.float32) * (convolved + skip_gain[None, :] * mixed_wide)).astype(
        jnp.bfloat16
    )


def solution(mesh):
    placed = (
        P(("outer", "inner"), None),
        P(("outer", "inner"), None),
        P(("outer", "inner"), None),
        P(("outer", "inner"), None),
        P(),
        P(),
    )
    return jax.shard_map(
        on_device,
        mesh=mesh,
        in_specs=placed,
        out_specs=P(("outer", "inner"), None),
        check_vma=False,
    )
```

```python
import math

import jax
import jax.numpy as jnp
from jax import lax
from jax.sharding import PartitionSpec as P
from jax.experimental import pallas as pl


def contract(pattern, left_op, right_op):
    return jnp.einsum(
        pattern,
        left_op,
        right_op,
        precision=lax.Precision.HIGH,
        preferred_element_type=jnp.float32,
    )


def angles_of(numerator, period):
    return 2.0 * math.pi / period * jnp.mod(numerator, period).astype(jnp.float32)


def dft_table(count_out, count_in, period):
    index_grid = (
        jnp.arange(count_out, dtype=jnp.int32)[:, None]
        * jnp.arange(count_in, dtype=jnp.int32)[None, :]
    )
    phases = angles_of(index_grid, period)
    return (jnp.cos(phases), jnp.sin(phases))


def rotate(real_part, imag_part, phases, direction):
    cosine = jnp.cos(phases)
    sine_part = jnp.sin(phases)
    if direction < 0:
        return (
            real_part * cosine + imag_part * sine_part,
            imag_part * cosine - real_part * sine_part,
        )
    return (real_part * cosine - imag_part * sine_part, imag_part * cosine + real_part * sine_part)


def transform(pattern, table_cos, table_sin, real_part, imag_part, direction):
    out_real = contract(pattern, table_cos, real_part) - direction * contract(
        pattern, table_sin, imag_part
    )
    out_imag = contract(pattern, table_cos, imag_part) + direction * contract(
        pattern, table_sin, real_part
    )
    return (out_real, out_imag)


def select_kernel(index_ref, filters_ref, out_ref):
    index = index_ref[...]
    groups = filters_ref.shape[1]
    onehot = (
        index == lax.broadcasted_iota(jnp.int32, (index.shape[0], groups), 1)
    ).astype(jnp.bfloat16)
    out_ref[...] = lax.dot_general(
        onehot,
        filters_ref[...],
        (((1,), (1,)), ((), ())),
        preferred_element_type=jnp.float32,
    ).astype(out_ref.dtype)


def select_filters(filters, group_index):
    channels = group_index.shape[0]
    return pl.pallas_call(
        select_kernel,
        out_shape=jax.ShapeDtypeStruct((channels, filters.shape[0]), jnp.bfloat16),
    )(group_index.reshape(channels, 1), filters)


def prep_kernel(key_ref, value_ref, filters_ref, index_ref, *out_refs):
    pieces = len(out_refs)
    n_dev, _, piece_width, _ = out_refs[0].shape
    mixed = (key_ref[...].astype(jnp.float32) * value_ref[...].astype(jnp.float32)).astype(
        jnp.bfloat16
    )
    mixed_t = mixed.astype(jnp.float32).T
    groups = filters_ref.shape[1]
    channels = index_ref.shape[1]
    onehot_t = (
        lax.broadcasted_iota(jnp.int32, (groups, channels), 0) == index_ref[...]
    ).astype(jnp.float32)
    picked = jnp.dot(
        filters_ref[...].astype(jnp.float32), onehot_t, preferred_element_type=jnp.float32
    ).T
    for dest in range(n_dev):
        for piece in range(pieces):
            low = (dest * pieces + piece) * piece_width
            out_refs[piece][dest, 0] = mixed_t[low : low + piece_width].astype(jnp.bfloat16)
            out_refs[piece][dest, 1] = picked[low : low + piece_width].astype(jnp.bfloat16)


def prepare(key_in, value_in, filters, group_index, n_dev, pieces):
    row_count, channels = key_in.shape
    piece_width = channels // (n_dev * pieces)
    return pl.pallas_call(
        prep_kernel,
        out_shape=tuple(
            jax.ShapeDtypeStruct((n_dev, 2, piece_width, row_count), jnp.bfloat16)
            for _ in range(pieces)
        ),
    )(key_in, value_in, filters, group_index.reshape(1, channels))


def finish_kernel(returned_ref, query_ref, key_ref, value_ref, gain_ref, out_ref):
    convolved = returned_ref[...].astype(jnp.float32).T
    mixed = (key_ref[...].astype(jnp.float32) * value_ref[...].astype(jnp.float32)).astype(
        jnp.bfloat16
    )
    out_ref[...] = (
        query_ref[...].astype(jnp.float32)
        * (convolved + gain_ref[...] * mixed.astype(jnp.float32))
    ).astype(out_ref.dtype)


def finish(returned, query, key_in, value_in, skip_gain):
    return pl.pallas_call(
        finish_kernel,
        out_shape=jax.ShapeDtypeStruct(query.shape, jnp.bfloat16),
    )(returned, query, key_in, value_in, skip_gain.reshape(1, -1))


def complex_table(cos_part, sin_part, direction):
    return jnp.concatenate(
        [
            jnp.concatenate([cos_part, direction * sin_part], axis=1),
            jnp.concatenate([-direction * sin_part, cos_part], axis=1),
        ],
        axis=0,
    )


def convolve_block(got, n_dev, row_count):
    own_width = got.shape[2]
    size_a = 2 * n_dev
    padded = size_a * row_count
    stacked = got.reshape(n_dev, 2 * own_width, row_count).astype(jnp.float32)
    first_cos, first_sin = dft_table(size_a, n_dev, size_a)
    first = contract("kn,ncb->kcb", jnp.concatenate([first_cos, -first_sin], axis=0), stacked)
    twiddle = angles_of(
        jnp.arange(size_a, dtype=jnp.int32)[:, None]
        * jnp.arange(row_count, dtype=jnp.int32)[None, :],
        padded,
    )[:, None, :]
    real_part, imag_part = rotate(first[:size_a], first[size_a:], twiddle, -1)
    second_cos, second_sin = dft_table(row_count, row_count, row_count)
    prod = contract(
        "kcb,bq->kcq",
        jnp.concatenate([real_part, imag_part], axis=2),
        complex_table(second_cos, second_sin, -1),
    )
    data_real = prod[:, :own_width, :row_count]
    data_imag = prod[:, :own_width, row_count:]
    filter_real = prod[:, own_width:, :row_count]
    filter_imag = prod[:, own_width:, row_count:]
    spec_real = data_real * filter_real - data_imag * filter_imag
    spec_imag = data_real * filter_imag + data_imag * filter_real
    prod = contract(
        "kcq,qb->kcb",
        jnp.concatenate([spec_real, spec_imag], axis=2),
        complex_table(second_cos, second_sin, 1),
    )
    real_part, imag_part = rotate(prod[:, :, :row_count], prod[:, :, row_count:], twiddle, 1)
    back_cos, back_sin = dft_table(n_dev, size_a, size_a)
    outcome = contract(
        "nk,kcb->ncb",
        jnp.concatenate([back_cos, -back_sin], axis=1),
        jnp.concatenate([real_part, imag_part], axis=0),
    )
    return (outcome * (1.0 / padded)).astype(jnp.bfloat16)


def by_channels(mixed, key_in, value_in, filters, group_index):
    n_dev = lax.axis_size("outer") * lax.axis_size("inner")
    row_count = mixed.shape[0]
    channels = mixed.shape[1]
    own_width = channels // n_dev
    pieces = 2 if own_width % 16 == 0 else 1
    piece_width = own_width // pieces
    if piece_width % 16 == 0:
        sent = prepare(key_in, value_in, filters, group_index, n_dev, pieces)
    else:
        chan_filters = select_filters(filters, group_index)
        sent = jnp.stack([mixed.T, chan_filters], axis=0).reshape(
            2, n_dev, pieces, piece_width, row_count
        )
        sent = sent.transpose(2, 1, 0, 3, 4)
    arrived = [
        lax.all_to_all(sent[piece], ("outer", "inner"), split_axis=0, concat_axis=0, tiled=True)
        for piece in range(pieces)
    ]
    results = []
    outcome = None
    for piece in range(pieces):
        got = arrived[piece]
        if outcome is not None:
            outcome, got = lax.optimization_barrier((outcome, got))
        outcome = convolve_block(got, n_dev, row_count)
        results.append(outcome)
    returned = lax.all_to_all(
        jnp.stack(results, axis=1), ("outer", "inner"), split_axis=0, concat_axis=0, tiled=True
    )
    return returned.reshape(channels, row_count)


def on_device(query, key_in, value_in, filters, group_index, skip_gain):
    mixed = (key_in.astype(jnp.float32) * value_in.astype(jnp.float32)).astype(jnp.bfloat16)
    returned = by_channels(mixed, key_in, value_in, filters, group_index)
    return finish(returned, query, key_in, value_in, skip_gain)


def solution(mesh):
    placed = (
        P(("outer", "inner"), None),
        P(("outer", "inner"), None),
        P(("outer", "inner"), None),
        P(("outer", "inner"), None),
        P(),
        P(),
    )
    return jax.shard_map(
        on_device,
        mesh=mesh,
        in_specs=placed,
        out_specs=P(("outer", "inner"), None),
        check_vma=False,
    )
```

```python
import math

import jax
import jax.numpy as jnp
from jax import lax
from jax.sharding import PartitionSpec as P
from jax.experimental import pallas as pl


def contract(pattern, left_op, right_op):
    return jnp.einsum(
        pattern,
        left_op,
        right_op,
        precision=lax.Precision.HIGH,
        preferred_element_type=jnp.float32,
    )


def angles_of(numerator, period):
    return 2.0 * math.pi / period * jnp.mod(numerator, period).astype(jnp.float32)


def dft_table(count_out, count_in, period):
    index_grid = (
        jnp.arange(count_out, dtype=jnp.int32)[:, None]
        * jnp.arange(count_in, dtype=jnp.int32)[None, :]
    )
    phases = angles_of(index_grid, period)
    return (jnp.cos(phases), jnp.sin(phases))


def rotate(real_part, imag_part, phases, direction):
    cosine = jnp.cos(phases)
    sine_part = jnp.sin(phases)
    if direction < 0:
        return (
            real_part * cosine + imag_part * sine_part,
            imag_part * cosine - real_part * sine_part,
        )
    return (real_part * cosine - imag_part * sine_part, imag_part * cosine + real_part * sine_part)


def transform(pattern, table_cos, table_sin, real_part, imag_part, direction):
    out_real = contract(pattern, table_cos, real_part) - direction * contract(
        pattern, table_sin, imag_part
    )
    out_imag = contract(pattern, table_cos, imag_part) + direction * contract(
        pattern, table_sin, real_part
    )
    return (out_real, out_imag)


def select_kernel(index_ref, filters_ref, out_ref):
    index = index_ref[...]
    groups = filters_ref.shape[1]
    onehot = (
        index == lax.broadcasted_iota(jnp.int32, (index.shape[0], groups), 1)
    ).astype(jnp.bfloat16)
    out_ref[...] = lax.dot_general(
        onehot,
        filters_ref[...],
        (((1,), (1,)), ((), ())),
        preferred_element_type=jnp.float32,
    ).astype(out_ref.dtype)


def select_filters(filters, group_index):
    channels = group_index.shape[0]
    return pl.pallas_call(
        select_kernel,
        out_shape=jax.ShapeDtypeStruct((channels, filters.shape[0]), jnp.bfloat16),
    )(group_index.reshape(channels, 1), filters)


def prep_kernel(key_ref, value_ref, filters_ref, index_ref, *out_refs):
    pieces = len(out_refs)
    n_local, _, piece_width, _ = out_refs[0].shape
    mixed = (key_ref[...].astype(jnp.float32) * value_ref[...].astype(jnp.float32)).astype(
        jnp.bfloat16
    )
    mixed_t = mixed.astype(jnp.float32).T
    groups = filters_ref.shape[1]
    channels = index_ref.shape[1]
    onehot_t = (
        lax.broadcasted_iota(jnp.int32, (groups, channels), 0) == index_ref[...]
    ).astype(jnp.float32)
    picked = jnp.dot(
        filters_ref[...].astype(jnp.float32), onehot_t, preferred_element_type=jnp.float32
    ).T
    for dest in range(n_local):
        for piece in range(pieces):
            low = (dest * pieces + piece) * piece_width
            out_refs[piece][dest, 0] = mixed_t[low : low + piece_width].astype(jnp.bfloat16)
            out_refs[piece][dest, 1] = picked[low : low + piece_width].astype(jnp.bfloat16)


def channel_block(channels, own_width):
    for size in (512, 256, 128):
        if channels % size == 0 and size % own_width == 0:
            return size
    return channels


def prepare(key_in, value_in, filters, group_index, n_dev, pieces):
    row_count, channels = key_in.shape
    own_width = channels // n_dev
    piece_width = own_width // pieces
    block = channel_block(channels, own_width)
    n_local = block // own_width
    return pl.pallas_call(
        prep_kernel,
        grid=(channels // block,),
        in_specs=[
            pl.BlockSpec((row_count, block), lambda i: (0, i)),
            pl.BlockSpec((row_count, block), lambda i: (0, i)),
            pl.BlockSpec(filters.shape, lambda i: (0, 0)),
            pl.BlockSpec((1, block), lambda i: (0, i)),
        ],
        out_specs=tuple(
            pl.BlockSpec((n_local, 2, piece_width, row_count), lambda i: (i, 0, 0, 0))
            for _ in range(pieces)
        ),
        out_shape=tuple(
            jax.ShapeDtypeStruct((n_dev, 2, piece_width, row_count), jnp.bfloat16)
            for _ in range(pieces)
        ),
    )(key_in, value_in, filters, group_index.reshape(1, channels))


def finish_kernel(returned_ref, query_ref, key_ref, value_ref, gain_ref, out_ref):
    convolved = returned_ref[...].astype(jnp.float32).T
    mixed = (key_ref[...].astype(jnp.float32) * value_ref[...].astype(jnp.float32)).astype(
        jnp.bfloat16
    )
    out_ref[...] = (
        query_ref[...].astype(jnp.float32)
        * (convolved + gain_ref[...] * mixed.astype(jnp.float32))
    ).astype(out_ref.dtype)


def finish(returned, query, key_in, value_in, skip_gain):
    row_count, channels = query.shape
    block = channel_block(channels, 128)
    row_spec = pl.BlockSpec((row_count, block), lambda i: (0, i))
    return pl.pallas_call(
        finish_kernel,
        grid=(channels // block,),
        in_specs=[
            pl.BlockSpec((block, row_count), lambda i: (i, 0)),
            row_spec,
            row_spec,
            row_spec,
            pl.BlockSpec((1, block), lambda i: (0, i)),
        ],
        out_specs=row_spec,
        out_shape=jax.ShapeDtypeStruct(query.shape, jnp.bfloat16),
    )(returned, query, key_in, value_in, skip_gain.reshape(1, -1))


def complex_table(cos_part, sin_part, direction):
    return jnp.concatenate(
        [
            jnp.concatenate([cos_part, direction * sin_part], axis=1),
            jnp.concatenate([-direction * sin_part, cos_part], axis=1),
        ],
        axis=0,
    )


def convolve_block(got, n_dev, row_count):
    own_width = got.shape[2]
    size_a = 2 * n_dev
    padded = size_a * row_count
    stacked = got.reshape(n_dev, 2 * own_width, row_count).astype(jnp.float32)
    first_cos, first_sin = dft_table(size_a, n_dev, size_a)
    first = contract("kn,ncb->kcb", jnp.concatenate([first_cos, -first_sin], axis=0), stacked)
    twiddle = angles_of(
        jnp.arange(size_a, dtype=jnp.int32)[:, None]
        * jnp.arange(row_count, dtype=jnp.int32)[None, :],
        padded,
    )[:, None, :]
    real_part, imag_part = rotate(first[:size_a], first[size_a:], twiddle, -1)
    second_cos, second_sin = dft_table(row_count, row_count, row_count)
    prod = contract(
        "kcb,bq->kcq",
        jnp.concatenate([real_part, imag_part], axis=2),
        complex_table(second_cos, second_sin, -1),
    )
    data_real = prod[:, :own_width, :row_count]
    data_imag = prod[:, :own_width, row_count:]
    filter_real = prod[:, own_width:, :row_count]
    filter_imag = prod[:, own_width:, row_count:]
    spec_real = data_real * filter_real - data_imag * filter_imag
    spec_imag = data_real * filter_imag + data_imag * filter_real
    prod = contract(
        "kcq,qb->kcb",
        jnp.concatenate([spec_real, spec_imag], axis=2),
        complex_table(second_cos, second_sin, 1),
    )
    real_part, imag_part = rotate(prod[:, :, :row_count], prod[:, :, row_count:], twiddle, 1)
    back_cos, back_sin = dft_table(n_dev, size_a, size_a)
    outcome = contract(
        "nk,kcb->ncb",
        jnp.concatenate([back_cos, -back_sin], axis=1),
        jnp.concatenate([real_part, imag_part], axis=0),
    )
    return (outcome * (1.0 / padded)).astype(jnp.bfloat16)


def by_channels(mixed, key_in, value_in, filters, group_index):
    n_dev = lax.axis_size("outer") * lax.axis_size("inner")
    row_count = mixed.shape[0]
    channels = mixed.shape[1]
    own_width = channels // n_dev
    pieces = 2 if own_width % 16 == 0 else 1
    piece_width = own_width // pieces
    if piece_width % 16 == 0:
        sent = prepare(key_in, value_in, filters, group_index, n_dev, pieces)
    else:
        chan_filters = select_filters(filters, group_index)
        sent = jnp.stack([mixed.T, chan_filters], axis=0).reshape(
            2, n_dev, pieces, piece_width, row_count
        )
        sent = sent.transpose(2, 1, 0, 3, 4)
    arrived = [
        lax.all_to_all(sent[piece], ("outer", "inner"), split_axis=0, concat_axis=0, tiled=True)
        for piece in range(pieces)
    ]
    results = []
    outcome = None
    for piece in range(pieces):
        got = arrived[piece]
        if outcome is not None:
            outcome, got = lax.optimization_barrier((outcome, got))
        outcome = convolve_block(got, n_dev, row_count)
        results.append(outcome)
    returned = lax.all_to_all(
        jnp.stack(results, axis=1), ("outer", "inner"), split_axis=0, concat_axis=0, tiled=True
    )
    return returned.reshape(channels, row_count)


def on_device(query, key_in, value_in, filters, group_index, skip_gain):
    mixed = (key_in.astype(jnp.float32) * value_in.astype(jnp.float32)).astype(jnp.bfloat16)
    returned = by_channels(mixed, key_in, value_in, filters, group_index)
    return finish(returned, query, key_in, value_in, skip_gain)


def solution(mesh):
    placed = (
        P(("outer", "inner"), None),
        P(("outer", "inner"), None),
        P(("outer", "inner"), None),
        P(("outer", "inner"), None),
        P(),
        P(),
    )
    return jax.shard_map(
        on_device,
        mesh=mesh,
        in_specs=placed,
        out_specs=P(("outer", "inner"), None),
        check_vma=False,
    )
```

```python
import math

import jax
import jax.numpy as jnp
from jax import lax
from jax.sharding import PartitionSpec as P
from jax.experimental import pallas as pl


def contract(pattern, left_op, right_op):
    return jnp.einsum(
        pattern,
        left_op,
        right_op,
        precision=lax.Precision.HIGH,
        preferred_element_type=jnp.float32,
    )


def angles_of(numerator, period):
    return 2.0 * math.pi / period * jnp.mod(numerator, period).astype(jnp.float32)


def dft_table(count_out, count_in, period):
    index_grid = (
        jnp.arange(count_out, dtype=jnp.int32)[:, None]
        * jnp.arange(count_in, dtype=jnp.int32)[None, :]
    )
    phases = angles_of(index_grid, period)
    return (jnp.cos(phases), jnp.sin(phases))


def rotate(real_part, imag_part, phases, direction):
    cosine = jnp.cos(phases)
    sine_part = jnp.sin(phases)
    if direction < 0:
        return (
            real_part * cosine + imag_part * sine_part,
            imag_part * cosine - real_part * sine_part,
        )
    return (real_part * cosine - imag_part * sine_part, imag_part * cosine + real_part * sine_part)


def transform(pattern, table_cos, table_sin, real_part, imag_part, direction):
    out_real = contract(pattern, table_cos, real_part) - direction * contract(
        pattern, table_sin, imag_part
    )
    out_imag = contract(pattern, table_cos, imag_part) + direction * contract(
        pattern, table_sin, real_part
    )
    return (out_real, out_imag)


def select_kernel(index_ref, filters_ref, out_ref):
    index = index_ref[...]
    groups = filters_ref.shape[1]
    onehot = (
        index == lax.broadcasted_iota(jnp.int32, (index.shape[0], groups), 1)
    ).astype(jnp.bfloat16)
    out_ref[...] = lax.dot_general(
        onehot,
        filters_ref[...],
        (((1,), (1,)), ((), ())),
        preferred_element_type=jnp.float32,
    ).astype(out_ref.dtype)


def select_filters(filters, group_index):
    channels = group_index.shape[0]
    return pl.pallas_call(
        select_kernel,
        out_shape=jax.ShapeDtypeStruct((channels, filters.shape[0]), jnp.bfloat16),
    )(group_index.reshape(channels, 1), filters)


def prep_kernel(key_ref, value_ref, filters_ref, index_ref, *out_refs):
    pieces = len(out_refs)
    n_dev, _, piece_width, _ = out_refs[0].shape
    mixed = (key_ref[...].astype(jnp.float32) * value_ref[...].astype(jnp.float32)).astype(
        jnp.bfloat16
    )
    mixed_t = mixed.astype(jnp.float32).T
    groups = filters_ref.shape[1]
    channels = index_ref.shape[1]
    onehot_t = (
        lax.broadcasted_iota(jnp.int32, (groups, channels), 0) == index_ref[...]
    ).astype(jnp.float32)
    picked = jnp.dot(
        filters_ref[...].astype(jnp.float32), onehot_t, preferred_element_type=jnp.float32
    ).T
    for dest in range(n_dev):
        for piece in range(pieces):
            low = (dest * pieces + piece) * piece_width
            out_refs[piece][dest, 0] = mixed_t[low : low + piece_width].astype(jnp.bfloat16)
            out_refs[piece][dest, 1] = picked[low : low + piece_width].astype(jnp.bfloat16)


def prepare(key_in, value_in, filters, group_index, n_dev, pieces):
    row_count, channels = key_in.shape
    piece_width = channels // (n_dev * pieces)
    return pl.pallas_call(
        prep_kernel,
        out_shape=tuple(
            jax.ShapeDtypeStruct((n_dev, 2, piece_width, row_count), jnp.bfloat16)
            for _ in range(pieces)
        ),
    )(key_in, value_in, filters, group_index.reshape(1, channels))


def finish_kernel(returned_ref, query_ref, key_ref, value_ref, gain_ref, out_ref):
    convolved = returned_ref[...].astype(jnp.float32).T
    mixed = (key_ref[...].astype(jnp.float32) * value_ref[...].astype(jnp.float32)).astype(
        jnp.bfloat16
    )
    out_ref[...] = (
        query_ref[...].astype(jnp.float32)
        * (convolved + gain_ref[...] * mixed.astype(jnp.float32))
    ).astype(out_ref.dtype)


def finish(returned, query, key_in, value_in, skip_gain):
    return pl.pallas_call(
        finish_kernel,
        out_shape=jax.ShapeDtypeStruct(query.shape, jnp.bfloat16),
    )(returned, query, key_in, value_in, skip_gain.reshape(1, -1))


def complex_table(cos_part, sin_part, direction):
    return jnp.concatenate(
        [
            jnp.concatenate([cos_part, direction * sin_part], axis=1),
            jnp.concatenate([-direction * sin_part, cos_part], axis=1),
        ],
        axis=0,
    )


def convolve_block(got, n_dev, row_count):
    own_width = got.shape[2]
    size_a = 2 * n_dev
    padded = size_a * row_count
    stacked = got.reshape(n_dev, 2 * own_width, row_count).astype(jnp.float32)
    first_cos, first_sin = dft_table(size_a, n_dev, size_a)
    first = contract("kn,ncb->kcb", jnp.concatenate([first_cos, -first_sin], axis=0), stacked)
    twiddle = angles_of(
        jnp.arange(size_a, dtype=jnp.int32)[:, None]
        * jnp.arange(row_count, dtype=jnp.int32)[None, :],
        padded,
    )[:, None, :]
    real_part, imag_part = rotate(first[:size_a], first[size_a:], twiddle, -1)
    second_cos, second_sin = dft_table(row_count, row_count, row_count)
    prod = contract(
        "kcb,bq->kcq",
        jnp.concatenate([real_part, imag_part], axis=2),
        complex_table(second_cos, second_sin, -1),
    )
    data_real = prod[:, :own_width, :row_count]
    data_imag = prod[:, :own_width, row_count:]
    filter_real = prod[:, own_width:, :row_count]
    filter_imag = prod[:, own_width:, row_count:]
    spec_real = data_real * filter_real - data_imag * filter_imag
    spec_imag = data_real * filter_imag + data_imag * filter_real
    prod = contract(
        "kcq,qb->kcb",
        jnp.concatenate([spec_real, spec_imag], axis=2),
        complex_table(second_cos, second_sin, 1),
    )
    real_part, imag_part = rotate(prod[:, :, :row_count], prod[:, :, row_count:], twiddle, 1)
    back_cos, back_sin = dft_table(n_dev, size_a, size_a)
    outcome = contract(
        "nk,kcb->ncb",
        jnp.concatenate([back_cos, -back_sin], axis=1),
        jnp.concatenate([real_part, imag_part], axis=0),
    )
    return (outcome * (1.0 / padded)).astype(jnp.bfloat16)


def by_channels(mixed, key_in, value_in, filters, group_index):
    n_dev = lax.axis_size("outer") * lax.axis_size("inner")
    row_count = mixed.shape[0]
    channels = mixed.shape[1]
    own_width = channels // n_dev
    pieces = 4 if own_width % 64 == 0 else (2 if own_width % 16 == 0 else 1)
    piece_width = own_width // pieces
    if piece_width % 16 == 0:
        sent = prepare(key_in, value_in, filters, group_index, n_dev, pieces)
    else:
        chan_filters = select_filters(filters, group_index)
        sent = jnp.stack([mixed.T, chan_filters], axis=0).reshape(
            2, n_dev, pieces, piece_width, row_count
        )
        sent = sent.transpose(2, 1, 0, 3, 4)
    arrived = [
        lax.all_to_all(sent[piece], ("outer", "inner"), split_axis=0, concat_axis=0, tiled=True)
        for piece in range(pieces)
    ]
    results = []
    outcome = None
    for piece in range(pieces):
        got = arrived[piece]
        if outcome is not None:
            outcome, got = lax.optimization_barrier((outcome, got))
        outcome = convolve_block(got, n_dev, row_count)
        results.append(outcome)
    returned = lax.all_to_all(
        jnp.stack(results, axis=1), ("outer", "inner"), split_axis=0, concat_axis=0, tiled=True
    )
    return returned.reshape(channels, row_count)


def on_device(query, key_in, value_in, filters, group_index, skip_gain):
    mixed = (key_in.astype(jnp.float32) * value_in.astype(jnp.float32)).astype(jnp.bfloat16)
    convolved = by_channels(mixed, key_in, value_in, filters, group_index).T.astype(jnp.float32)
    mixed_wide = mixed.astype(jnp.float32)
    return (query.astype(jnp.float32) * (convolved + skip_gain[None, :] * mixed_wide)).astype(
        jnp.bfloat16
    )


def solution(mesh):
    placed = (
        P(("outer", "inner"), None),
        P(("outer", "inner"), None),
        P(("outer", "inner"), None),
        P(("outer", "inner"), None),
        P(),
        P(),
    )
    return jax.shard_map(
        on_device,
        mesh=mesh,
        in_specs=placed,
        out_specs=P(("outer", "inner"), None),
        check_vma=False,
    )
```

```python
import math

import jax
import jax.numpy as jnp
from jax import lax
from jax.sharding import PartitionSpec as P
from jax.experimental import pallas as pl


def contract(pattern, left_op, right_op):
    return jnp.einsum(
        pattern,
        left_op,
        right_op,
        precision=lax.Precision.HIGH,
        preferred_element_type=jnp.float32,
    )


def angles_of(numerator, period):
    return 2.0 * math.pi / period * jnp.mod(numerator, period).astype(jnp.float32)


def dft_table(count_out, count_in, period):
    index_grid = (
        jnp.arange(count_out, dtype=jnp.int32)[:, None]
        * jnp.arange(count_in, dtype=jnp.int32)[None, :]
    )
    phases = angles_of(index_grid, period)
    return (jnp.cos(phases), jnp.sin(phases))


def rotate(real_part, imag_part, phases, direction):
    cosine = jnp.cos(phases)
    sine_part = jnp.sin(phases)
    if direction < 0:
        return (
            real_part * cosine + imag_part * sine_part,
            imag_part * cosine - real_part * sine_part,
        )
    return (real_part * cosine - imag_part * sine_part, imag_part * cosine + real_part * sine_part)


def transform(pattern, table_cos, table_sin, real_part, imag_part, direction):
    out_real = contract(pattern, table_cos, real_part) - direction * contract(
        pattern, table_sin, imag_part
    )
    out_imag = contract(pattern, table_cos, imag_part) + direction * contract(
        pattern, table_sin, real_part
    )
    return (out_real, out_imag)


def select_kernel(index_ref, filters_ref, out_ref):
    index = index_ref[...]
    groups = filters_ref.shape[1]
    onehot = (
        index == lax.broadcasted_iota(jnp.int32, (index.shape[0], groups), 1)
    ).astype(jnp.bfloat16)
    out_ref[...] = lax.dot_general(
        onehot,
        filters_ref[...],
        (((1,), (1,)), ((), ())),
        preferred_element_type=jnp.float32,
    ).astype(out_ref.dtype)


def select_filters(filters, group_index):
    channels = group_index.shape[0]
    return pl.pallas_call(
        select_kernel,
        out_shape=jax.ShapeDtypeStruct((channels, filters.shape[0]), jnp.bfloat16),
    )(group_index.reshape(channels, 1), filters)


def prep_kernel(key_ref, value_ref, filters_ref, index_ref, *out_refs):
    pieces = len(out_refs)
    n_dev, _, piece_width, _ = out_refs[0].shape
    mixed = (key_ref[...].astype(jnp.float32) * value_ref[...].astype(jnp.float32)).astype(
        jnp.bfloat16
    )
    mixed_t = mixed.astype(jnp.float32).T
    groups = filters_ref.shape[1]
    channels = index_ref.shape[1]
    onehot_t = (
        lax.broadcasted_iota(jnp.int32, (groups, channels), 0) == index_ref[...]
    ).astype(jnp.float32)
    picked = jnp.dot(
        filters_ref[...].astype(jnp.float32), onehot_t, preferred_element_type=jnp.float32
    ).T
    for dest in range(n_dev):
        for piece in range(pieces):
            low = (dest * pieces + piece) * piece_width
            out_refs[piece][dest, 0] = mixed_t[low : low + piece_width].astype(jnp.bfloat16)
            out_refs[piece][dest, 1] = picked[low : low + piece_width].astype(jnp.bfloat16)


def prepare(key_in, value_in, filters, group_index, n_dev, pieces):
    row_count, channels = key_in.shape
    piece_width = channels // (n_dev * pieces)
    return pl.pallas_call(
        prep_kernel,
        out_shape=tuple(
            jax.ShapeDtypeStruct((n_dev, 2, piece_width, row_count), jnp.bfloat16)
            for _ in range(pieces)
        ),
    )(key_in, value_in, filters, group_index.reshape(1, channels))


def finish_kernel(returned_ref, query_ref, key_ref, value_ref, gain_ref, out_ref):
    convolved = returned_ref[...].astype(jnp.float32).T
    mixed = (key_ref[...].astype(jnp.float32) * value_ref[...].astype(jnp.float32)).astype(
        jnp.bfloat16
    )
    out_ref[...] = (
        query_ref[...].astype(jnp.float32)
        * (convolved + gain_ref[...] * mixed.astype(jnp.float32))
    ).astype(out_ref.dtype)


def finish(returned, query, key_in, value_in, skip_gain):
    return pl.pallas_call(
        finish_kernel,
        out_shape=jax.ShapeDtypeStruct(query.shape, jnp.bfloat16),
    )(returned, query, key_in, value_in, skip_gain.reshape(1, -1))


def complex_table(cos_part, sin_part, direction):
    return jnp.concatenate(
        [
            jnp.concatenate([cos_part, direction * sin_part], axis=1),
            jnp.concatenate([-direction * sin_part, cos_part], axis=1),
        ],
        axis=0,
    )


def convolve_block(got, n_dev, row_count):
    own_width = got.shape[2]
    size_a = 2 * n_dev
    kept = n_dev + 1
    padded = size_a * row_count
    stacked = got.reshape(n_dev, 2 * own_width, row_count).astype(jnp.float32)
    first_cos, first_sin = dft_table(kept, n_dev, size_a)
    first = contract("kn,ncb->kcb", jnp.concatenate([first_cos, -first_sin], axis=0), stacked)
    twiddle = angles_of(
        jnp.arange(kept, dtype=jnp.int32)[:, None]
        * jnp.arange(row_count, dtype=jnp.int32)[None, :],
        padded,
    )[:, None, :]
    real_part, imag_part = rotate(first[:kept], first[kept:], twiddle, -1)
    second_cos, second_sin = dft_table(row_count, row_count, row_count)
    prod = contract(
        "kcb,bq->kcq",
        jnp.concatenate([real_part, imag_part], axis=2),
        complex_table(second_cos, second_sin, -1),
    )
    data_real = prod[:, :own_width, :row_count]
    data_imag = prod[:, :own_width, row_count:]
    filter_real = prod[:, own_width:, :row_count]
    filter_imag = prod[:, own_width:, row_count:]
    spec_real = data_real * filter_real - data_imag * filter_imag
    spec_imag = data_real * filter_imag + data_imag * filter_real
    prod = contract(
        "kcq,qb->kcb",
        jnp.concatenate([spec_real, spec_imag], axis=2),
        complex_table(second_cos, second_sin, 1),
    )
    real_part, imag_part = rotate(prod[:, :, :row_count], prod[:, :, row_count:], twiddle, 1)
    back_cos, back_sin = dft_table(n_dev, kept, size_a)
    index = jnp.arange(kept)
    weight = jnp.where((index == 0) | (index == n_dev), 1.0, 2.0).astype(jnp.float32)[None, :]
    outcome = contract(
        "nk,kcb->ncb",
        jnp.concatenate([back_cos * weight, -back_sin * weight], axis=1),
        jnp.concatenate([real_part, imag_part], axis=0),
    )
    return (outcome * (1.0 / padded)).astype(jnp.bfloat16)


def by_channels(mixed, key_in, value_in, filters, group_index):
    n_dev = lax.axis_size("outer") * lax.axis_size("inner")
    row_count = mixed.shape[0]
    channels = mixed.shape[1]
    own_width = channels // n_dev
    pieces = 2 if own_width % 16 == 0 else 1
    piece_width = own_width // pieces
    if piece_width % 16 == 0:
        sent = prepare(key_in, value_in, filters, group_index, n_dev, pieces)
    else:
        chan_filters = select_filters(filters, group_index)
        sent = jnp.stack([mixed.T, chan_filters], axis=0).reshape(
            2, n_dev, pieces, piece_width, row_count
        )
        sent = sent.transpose(2, 1, 0, 3, 4)
    arrived = [
        lax.all_to_all(sent[piece], ("outer", "inner"), split_axis=0, concat_axis=0, tiled=True)
        for piece in range(pieces)
    ]
    results = []
    outcome = None
    for piece in range(pieces):
        got = arrived[piece]
        if outcome is not None:
            outcome, got = lax.optimization_barrier((outcome, got))
        outcome = convolve_block(got, n_dev, row_count)
        results.append(outcome)
    returned = lax.all_to_all(
        jnp.stack(results, axis=1), ("outer", "inner"), split_axis=0, concat_axis=0, tiled=True
    )
    return returned.reshape(channels, row_count)


def on_device(query, key_in, value_in, filters, group_index, skip_gain):
    mixed = (key_in.astype(jnp.float32) * value_in.astype(jnp.float32)).astype(jnp.bfloat16)
    convolved = by_channels(mixed, key_in, value_in, filters, group_index).T.astype(jnp.float32)
    mixed_wide = mixed.astype(jnp.float32)
    return (query.astype(jnp.float32) * (convolved + skip_gain[None, :] * mixed_wide)).astype(
        jnp.bfloat16
    )


def solution(mesh):
    placed = (
        P(("outer", "inner"), None),
        P(("outer", "inner"), None),
        P(("outer", "inner"), None),
        P(("outer", "inner"), None),
        P(),
        P(),
    )
    return jax.shard_map(
        on_device,
        mesh=mesh,
        in_specs=placed,
        out_specs=P(("outer", "inner"), None),
        check_vma=False,
    )
```

```python
import math

import jax
import jax.numpy as jnp
from jax import lax
from jax.sharding import PartitionSpec as P
from jax.experimental import pallas as pl


def contract(pattern, left_op, right_op):
    return jnp.einsum(
        pattern,
        left_op,
        right_op,
        precision=lax.Precision.HIGH,
        preferred_element_type=jnp.float32,
    )


def angles_of(numerator, period):
    return 2.0 * math.pi / period * jnp.mod(numerator, period).astype(jnp.float32)


def dft_table(count_out, count_in, period):
    index_grid = (
        jnp.arange(count_out, dtype=jnp.int32)[:, None]
        * jnp.arange(count_in, dtype=jnp.int32)[None, :]
    )
    phases = angles_of(index_grid, period)
    return (jnp.cos(phases), jnp.sin(phases))


def rotate(real_part, imag_part, phases, direction):
    cosine = jnp.cos(phases)
    sine_part = jnp.sin(phases)
    if direction < 0:
        return (
            real_part * cosine + imag_part * sine_part,
            imag_part * cosine - real_part * sine_part,
        )
    return (real_part * cosine - imag_part * sine_part, imag_part * cosine + real_part * sine_part)


def transform(pattern, table_cos, table_sin, real_part, imag_part, direction):
    out_real = contract(pattern, table_cos, real_part) - direction * contract(
        pattern, table_sin, imag_part
    )
    out_imag = contract(pattern, table_cos, imag_part) + direction * contract(
        pattern, table_sin, real_part
    )
    return (out_real, out_imag)


def select_kernel(index_ref, filters_ref, out_ref):
    index = index_ref[...]
    groups = filters_ref.shape[1]
    onehot = (
        index == lax.broadcasted_iota(jnp.int32, (index.shape[0], groups), 1)
    ).astype(jnp.bfloat16)
    out_ref[...] = lax.dot_general(
        onehot,
        filters_ref[...],
        (((1,), (1,)), ((), ())),
        preferred_element_type=jnp.float32,
    ).astype(out_ref.dtype)


def select_filters(filters, group_index):
    channels = group_index.shape[0]
    return pl.pallas_call(
        select_kernel,
        out_shape=jax.ShapeDtypeStruct((channels, filters.shape[0]), jnp.bfloat16),
    )(group_index.reshape(channels, 1), filters)


def prep_kernel(key_ref, value_ref, filters_ref, index_ref, *out_refs):
    pieces = len(out_refs)
    n_dev, _, piece_width, _ = out_refs[0].shape
    mixed = (key_ref[...].astype(jnp.float32) * value_ref[...].astype(jnp.float32)).astype(
        jnp.bfloat16
    )
    mixed_t = mixed.astype(jnp.float32).T
    groups = filters_ref.shape[1]
    channels = index_ref.shape[1]
    onehot_t = (
        lax.broadcasted_iota(jnp.int32, (groups, channels), 0) == index_ref[...]
    ).astype(jnp.float32)
    picked = jnp.dot(
        filters_ref[...].astype(jnp.float32), onehot_t, preferred_element_type=jnp.float32
    ).T
    for dest in range(n_dev):
        for piece in range(pieces):
            low = (dest * pieces + piece) * piece_width
            out_refs[piece][dest, 0] = mixed_t[low : low + piece_width].astype(jnp.bfloat16)
            out_refs[piece][dest, 1] = picked[low : low + piece_width].astype(jnp.bfloat16)


def prepare(key_in, value_in, filters, group_index, n_dev, pieces):
    row_count, channels = key_in.shape
    piece_width = channels // (n_dev * pieces)
    return pl.pallas_call(
        prep_kernel,
        out_shape=tuple(
            jax.ShapeDtypeStruct((n_dev, 2, piece_width, row_count), jnp.bfloat16)
            for _ in range(pieces)
        ),
    )(key_in, value_in, filters, group_index.reshape(1, channels))


def finish_kernel(returned_ref, query_ref, key_ref, value_ref, gain_ref, out_ref):
    convolved = returned_ref[...].astype(jnp.float32).T
    mixed = (key_ref[...].astype(jnp.float32) * value_ref[...].astype(jnp.float32)).astype(
        jnp.bfloat16
    )
    out_ref[...] = (
        query_ref[...].astype(jnp.float32)
        * (convolved + gain_ref[...] * mixed.astype(jnp.float32))
    ).astype(out_ref.dtype)


def finish(returned, query, key_in, value_in, skip_gain):
    return pl.pallas_call(
        finish_kernel,
        out_shape=jax.ShapeDtypeStruct(query.shape, jnp.bfloat16),
    )(returned, query, key_in, value_in, skip_gain.reshape(1, -1))


def complex_table(cos_part, sin_part, direction):
    return jnp.concatenate(
        [
            jnp.concatenate([cos_part, direction * sin_part], axis=1),
            jnp.concatenate([-direction * sin_part, cos_part], axis=1),
        ],
        axis=0,
    )


def convolve_block(got, n_dev, row_count):
    own_width = got.shape[2]
    size_a = 2 * n_dev
    kept = n_dev + 1
    padded = size_a * row_count
    stacked = got.reshape(n_dev, 2 * own_width, row_count).astype(jnp.float32)
    first_cos, first_sin = dft_table(kept, n_dev, size_a)
    first = contract("kn,ncb->kcb", jnp.concatenate([first_cos, -first_sin], axis=0), stacked)
    twiddle = angles_of(
        jnp.arange(kept, dtype=jnp.int32)[:, None]
        * jnp.arange(row_count, dtype=jnp.int32)[None, :],
        padded,
    )[:, None, :]
    real_part, imag_part = rotate(first[:kept], first[kept:], twiddle, -1)
    second_cos, second_sin = dft_table(row_count, row_count, row_count)
    prod = contract(
        "kcb,bq->kcq",
        jnp.concatenate([real_part, imag_part], axis=2),
        complex_table(second_cos, second_sin, -1),
    )
    data_real = prod[:, :own_width, :row_count]
    data_imag = prod[:, :own_width, row_count:]
    filter_real = prod[:, own_width:, :row_count]
    filter_imag = prod[:, own_width:, row_count:]
    spec_real = data_real * filter_real - data_imag * filter_imag
    spec_imag = data_real * filter_imag + data_imag * filter_real
    prod = contract(
        "kcq,qb->kcb",
        jnp.concatenate([spec_real, spec_imag], axis=2),
        complex_table(second_cos, second_sin, 1),
    )
    real_part, imag_part = rotate(prod[:, :, :row_count], prod[:, :, row_count:], twiddle, 1)
    back_cos, back_sin = dft_table(n_dev, kept, size_a)
    index = jnp.arange(kept)
    weight = jnp.where((index == 0) | (index == n_dev), 1.0, 2.0).astype(jnp.float32)[None, :]
    outcome = contract(
        "nk,kcb->ncb",
        jnp.concatenate([back_cos * weight, -back_sin * weight], axis=1),
        jnp.concatenate([real_part, imag_part], axis=0),
    )
    return (outcome * (1.0 / padded)).astype(jnp.bfloat16)


def by_channels(mixed, key_in, value_in, filters, group_index):
    n_dev = lax.axis_size("outer") * lax.axis_size("inner")
    row_count = mixed.shape[0]
    channels = mixed.shape[1]
    own_width = channels // n_dev
    pieces = 1
    piece_width = own_width // pieces
    if piece_width % 16 == 0:
        sent = prepare(key_in, value_in, filters, group_index, n_dev, pieces)
    else:
        chan_filters = select_filters(filters, group_index)
        sent = jnp.stack([mixed.T, chan_filters], axis=0).reshape(
            2, n_dev, pieces, piece_width, row_count
        )
        sent = sent.transpose(2, 1, 0, 3, 4)
    arrived = [
        lax.all_to_all(sent[piece], ("outer", "inner"), split_axis=0, concat_axis=0, tiled=True)
        for piece in range(pieces)
    ]
    results = []
    outcome = None
    for piece in range(pieces):
        got = arrived[piece]
        if outcome is not None:
            outcome, got = lax.optimization_barrier((outcome, got))
        outcome = convolve_block(got, n_dev, row_count)
        results.append(outcome)
    returned = lax.all_to_all(
        jnp.stack(results, axis=1), ("outer", "inner"), split_axis=0, concat_axis=0, tiled=True
    )
    return returned.reshape(channels, row_count)


def on_device(query, key_in, value_in, filters, group_index, skip_gain):
    mixed = (key_in.astype(jnp.float32) * value_in.astype(jnp.float32)).astype(jnp.bfloat16)
    convolved = by_channels(mixed, key_in, value_in, filters, group_index).T.astype(jnp.float32)
    mixed_wide = mixed.astype(jnp.float32)
    return (query.astype(jnp.float32) * (convolved + skip_gain[None, :] * mixed_wide)).astype(
        jnp.bfloat16
    )


def solution(mesh):
    placed = (
        P(("outer", "inner"), None),
        P(("outer", "inner"), None),
        P(("outer", "inner"), None),
        P(("outer", "inner"), None),
        P(),
        P(),
    )
    return jax.shard_map(
        on_device,
        mesh=mesh,
        in_specs=placed,
        out_specs=P(("outer", "inner"), None),
        check_vma=False,
    )
```

```python
import math

import jax
import jax.numpy as jnp
from jax import lax
from jax.sharding import PartitionSpec as P
from jax.experimental import pallas as pl


def contract(pattern, left_op, right_op):
    return jnp.einsum(
        pattern,
        left_op,
        right_op,
        precision=lax.Precision.HIGH,
        preferred_element_type=jnp.float32,
    )


def angles_of(numerator, period):
    return 2.0 * math.pi / period * jnp.mod(numerator, period).astype(jnp.float32)


def dft_table(count_out, count_in, period):
    index_grid = (
        jnp.arange(count_out, dtype=jnp.int32)[:, None]
        * jnp.arange(count_in, dtype=jnp.int32)[None, :]
    )
    phases = angles_of(index_grid, period)
    return (jnp.cos(phases), jnp.sin(phases))


def rotate(real_part, imag_part, phases, direction):
    cosine = jnp.cos(phases)
    sine_part = jnp.sin(phases)
    if direction < 0:
        return (
            real_part * cosine + imag_part * sine_part,
            imag_part * cosine - real_part * sine_part,
        )
    return (real_part * cosine - imag_part * sine_part, imag_part * cosine + real_part * sine_part)


def transform(pattern, table_cos, table_sin, real_part, imag_part, direction):
    out_real = contract(pattern, table_cos, real_part) - direction * contract(
        pattern, table_sin, imag_part
    )
    out_imag = contract(pattern, table_cos, imag_part) + direction * contract(
        pattern, table_sin, real_part
    )
    return (out_real, out_imag)


def select_kernel(index_ref, filters_ref, out_ref):
    index = index_ref[...]
    groups = filters_ref.shape[1]
    onehot = (
        index == lax.broadcasted_iota(jnp.int32, (index.shape[0], groups), 1)
    ).astype(jnp.bfloat16)
    out_ref[...] = lax.dot_general(
        onehot,
        filters_ref[...],
        (((1,), (1,)), ((), ())),
        preferred_element_type=jnp.float32,
    ).astype(out_ref.dtype)


def select_filters(filters, group_index):
    channels = group_index.shape[0]
    return pl.pallas_call(
        select_kernel,
        out_shape=jax.ShapeDtypeStruct((channels, filters.shape[0]), jnp.bfloat16),
    )(group_index.reshape(channels, 1), filters)


def prep_kernel(key_ref, value_ref, filters_ref, index_ref, *out_refs):
    pieces = len(out_refs)
    n_dev, _, piece_width, _ = out_refs[0].shape
    mixed = (key_ref[...].astype(jnp.float32) * value_ref[...].astype(jnp.float32)).astype(
        jnp.bfloat16
    )
    mixed_t = mixed.astype(jnp.float32).T
    groups = filters_ref.shape[1]
    channels = index_ref.shape[1]
    onehot_t = (
        lax.broadcasted_iota(jnp.int32, (groups, channels), 0) == index_ref[...]
    ).astype(jnp.float32)
    picked = jnp.dot(
        filters_ref[...].astype(jnp.float32), onehot_t, preferred_element_type=jnp.float32
    ).T
    for dest in range(n_dev):
        for piece in range(pieces):
            low = (dest * pieces + piece) * piece_width
            out_refs[piece][dest, 0] = mixed_t[low : low + piece_width].astype(jnp.bfloat16)
            out_refs[piece][dest, 1] = picked[low : low + piece_width].astype(jnp.bfloat16)


def prepare(key_in, value_in, filters, group_index, n_dev, pieces):
    row_count, channels = key_in.shape
    piece_width = channels // (n_dev * pieces)
    return pl.pallas_call(
        prep_kernel,
        out_shape=tuple(
            jax.ShapeDtypeStruct((n_dev, 2, piece_width, row_count), jnp.bfloat16)
            for _ in range(pieces)
        ),
    )(key_in, value_in, filters, group_index.reshape(1, channels))


def finish_kernel(returned_ref, query_ref, key_ref, value_ref, gain_ref, out_ref):
    convolved = returned_ref[...].astype(jnp.float32).T
    mixed = (key_ref[...].astype(jnp.float32) * value_ref[...].astype(jnp.float32)).astype(
        jnp.bfloat16
    )
    out_ref[...] = (
        query_ref[...].astype(jnp.float32)
        * (convolved + gain_ref[...] * mixed.astype(jnp.float32))
    ).astype(out_ref.dtype)


def finish(returned, query, key_in, value_in, skip_gain):
    return pl.pallas_call(
        finish_kernel,
        out_shape=jax.ShapeDtypeStruct(query.shape, jnp.bfloat16),
    )(returned, query, key_in, value_in, skip_gain.reshape(1, -1))


def complex_table(cos_part, sin_part, direction):
    return jnp.concatenate(
        [
            jnp.concatenate([cos_part, direction * sin_part], axis=1),
            jnp.concatenate([-direction * sin_part, cos_part], axis=1),
        ],
        axis=0,
    )


def convolve_block(got, n_dev, row_count):
    own_width = got.shape[2]
    size_a = 2 * n_dev
    kept = n_dev + 1
    padded = size_a * row_count
    stacked = got.reshape(n_dev, 2 * own_width, row_count)
    first_cos, first_sin = dft_table(kept, n_dev, size_a)
    first_table = jnp.concatenate([first_cos, -first_sin], axis=0)
    table_high = first_table.astype(jnp.bfloat16)
    table_low = (first_table - table_high.astype(jnp.float32)).astype(jnp.bfloat16)
    first = jnp.einsum(
        "kn,ncb->kcb", table_high, stacked, preferred_element_type=jnp.float32
    ) + jnp.einsum("kn,ncb->kcb", table_low, stacked, preferred_element_type=jnp.float32)
    twiddle = angles_of(
        jnp.arange(kept, dtype=jnp.int32)[:, None]
        * jnp.arange(row_count, dtype=jnp.int32)[None, :],
        padded,
    )[:, None, :]
    real_part, imag_part = rotate(first[:kept], first[kept:], twiddle, -1)
    second_cos, second_sin = dft_table(row_count, row_count, row_count)
    prod = contract(
        "kcb,bq->kcq",
        jnp.concatenate([real_part, imag_part], axis=2),
        complex_table(second_cos, second_sin, -1),
    )
    data_real = prod[:, :own_width, :row_count]
    data_imag = prod[:, :own_width, row_count:]
    filter_real = prod[:, own_width:, :row_count]
    filter_imag = prod[:, own_width:, row_count:]
    spec_real = data_real * filter_real - data_imag * filter_imag
    spec_imag = data_real * filter_imag + data_imag * filter_real
    prod = contract(
        "kcq,qb->kcb",
        jnp.concatenate([spec_real, spec_imag], axis=2),
        complex_table(second_cos, second_sin, 1),
    )
    real_part, imag_part = rotate(prod[:, :, :row_count], prod[:, :, row_count:], twiddle, 1)
    back_cos, back_sin = dft_table(n_dev, kept, size_a)
    index = jnp.arange(kept)
    weight = jnp.where((index == 0) | (index == n_dev), 1.0, 2.0).astype(jnp.float32)[None, :]
    outcome = contract(
        "nk,kcb->ncb",
        jnp.concatenate([back_cos * weight, -back_sin * weight], axis=1),
        jnp.concatenate([real_part, imag_part], axis=0),
    )
    return (outcome * (1.0 / padded)).astype(jnp.bfloat16)


def exchange(blocks, n_dev, me):
    axes = ("outer", "inner")
    arrived = [blocks[me][None]]
    for shift in range(1, n_dev):
        part = lax.dynamic_index_in_dim(blocks, (me + shift) % n_dev, axis=0)
        arrived.append(
            lax.ppermute(part, axes, perm=[(d, (d + shift) % n_dev) for d in range(n_dev)])
        )
    reversed_order = jnp.concatenate([arrived[0]] + arrived[:0:-1], axis=0)
    doubled = jnp.concatenate([reversed_order, reversed_order], axis=0)
    return lax.dynamic_slice_in_dim(doubled, (n_dev - me) % n_dev, n_dev, axis=0)


def by_channels(mixed, key_in, value_in, filters, group_index):
    n_dev = lax.axis_size("outer") * lax.axis_size("inner")
    row_count = mixed.shape[0]
    channels = mixed.shape[1]
    own_width = channels // n_dev
    pieces = 1
    piece_width = own_width // pieces
    if piece_width % 16 == 0:
        sent = prepare(key_in, value_in, filters, group_index, n_dev, pieces)
    else:
        chan_filters = select_filters(filters, group_index)
        sent = jnp.stack([mixed.T, chan_filters], axis=0).reshape(
            2, n_dev, pieces, piece_width, row_count
        )
        sent = sent.transpose(2, 1, 0, 3, 4)
    arrived = [
        lax.all_to_all(sent[piece], ("outer", "inner"), split_axis=0, concat_axis=0, tiled=True)
        for piece in range(pieces)
    ]
    results = []
    outcome = None
    for piece in range(pieces):
        got = arrived[piece]
        if outcome is not None:
            outcome, got = lax.optimization_barrier((outcome, got))
        outcome = convolve_block(got, n_dev, row_count)
        results.append(outcome)
    me = lax.axis_index("outer") * lax.axis_size("inner") + lax.axis_index("inner")
    if n_dev <= 32:
        returned = exchange(jnp.stack(results, axis=1), n_dev, me)
    else:
        returned = lax.all_to_all(
            jnp.stack(results, axis=1), ("outer", "inner"), split_axis=0, concat_axis=0, tiled=True
        )
    return returned.reshape(channels, row_count)


def on_device(query, key_in, value_in, filters, group_index, skip_gain):
    mixed = (key_in.astype(jnp.float32) * value_in.astype(jnp.float32)).astype(jnp.bfloat16)
    convolved = by_channels(mixed, key_in, value_in, filters, group_index).T.astype(jnp.float32)
    mixed_wide = mixed.astype(jnp.float32)
    return (query.astype(jnp.float32) * (convolved + skip_gain[None, :] * mixed_wide)).astype(
        jnp.bfloat16
    )


def solution(mesh):
    placed = (
        P(("outer", "inner"), None),
        P(("outer", "inner"), None),
        P(("outer", "inner"), None),
        P(("outer", "inner"), None),
        P(),
        P(),
    )
    return jax.shard_map(
        on_device,
        mesh=mesh,
        in_specs=placed,
        out_specs=P(("outer", "inner"), None),
        check_vma=False,
    )
```

```python
import math

import jax
import jax.numpy as jnp
from jax import lax
from jax.sharding import PartitionSpec as P
from jax.experimental import pallas as pl


def contract(pattern, left_op, right_op):
    return jnp.einsum(
        pattern,
        left_op,
        right_op,
        precision=lax.Precision.HIGH,
        preferred_element_type=jnp.float32,
    )


def angles_of(numerator, period):
    return 2.0 * math.pi / period * jnp.mod(numerator, period).astype(jnp.float32)


def dft_table(count_out, count_in, period):
    index_grid = (
        jnp.arange(count_out, dtype=jnp.int32)[:, None]
        * jnp.arange(count_in, dtype=jnp.int32)[None, :]
    )
    phases = angles_of(index_grid, period)
    return (jnp.cos(phases), jnp.sin(phases))


def rotate(real_part, imag_part, phases, direction):
    cosine = jnp.cos(phases)
    sine_part = jnp.sin(phases)
    if direction < 0:
        return (
            real_part * cosine + imag_part * sine_part,
            imag_part * cosine - real_part * sine_part,
        )
    return (real_part * cosine - imag_part * sine_part, imag_part * cosine + real_part * sine_part)


def transform(pattern, table_cos, table_sin, real_part, imag_part, direction):
    out_real = contract(pattern, table_cos, real_part) - direction * contract(
        pattern, table_sin, imag_part
    )
    out_imag = contract(pattern, table_cos, imag_part) + direction * contract(
        pattern, table_sin, real_part
    )
    return (out_real, out_imag)


def select_kernel(index_ref, filters_ref, out_ref):
    index = index_ref[...]
    groups = filters_ref.shape[1]
    onehot = (
        index == lax.broadcasted_iota(jnp.int32, (index.shape[0], groups), 1)
    ).astype(jnp.bfloat16)
    out_ref[...] = lax.dot_general(
        onehot,
        filters_ref[...],
        (((1,), (1,)), ((), ())),
        preferred_element_type=jnp.float32,
    ).astype(out_ref.dtype)


def select_filters(filters, group_index):
    channels = group_index.shape[0]
    return pl.pallas_call(
        select_kernel,
        out_shape=jax.ShapeDtypeStruct((channels, filters.shape[0]), jnp.bfloat16),
    )(group_index.reshape(channels, 1), filters)


def prep_kernel(key_ref, value_ref, filters_ref, index_ref, *out_refs):
    pieces = len(out_refs)
    n_dev, _, piece_width, _ = out_refs[0].shape
    mixed = (key_ref[...].astype(jnp.float32) * value_ref[...].astype(jnp.float32)).astype(
        jnp.bfloat16
    )
    mixed_t = mixed.astype(jnp.float32).T
    groups = filters_ref.shape[1]
    channels = index_ref.shape[1]
    onehot_t = (
        lax.broadcasted_iota(jnp.int32, (groups, channels), 0) == index_ref[...]
    ).astype(jnp.bfloat16)
    picked = jnp.dot(filters_ref[...], onehot_t, preferred_element_type=jnp.float32).T
    for dest in range(n_dev):
        for piece in range(pieces):
            low = (dest * pieces + piece) * piece_width
            out_refs[piece][dest, 0] = mixed_t[low : low + piece_width].astype(jnp.bfloat16)
            out_refs[piece][dest, 1] = picked[low : low + piece_width].astype(jnp.bfloat16)


def prepare(key_in, value_in, filters, group_index, n_dev, pieces):
    row_count, channels = key_in.shape
    piece_width = channels // (n_dev * pieces)
    return pl.pallas_call(
        prep_kernel,
        out_shape=tuple(
            jax.ShapeDtypeStruct((n_dev, 2, piece_width, row_count), jnp.bfloat16)
            for _ in range(pieces)
        ),
    )(key_in, value_in, filters, group_index.reshape(1, channels))


def finish_kernel(returned_ref, query_ref, key_ref, value_ref, gain_ref, out_ref):
    convolved = returned_ref[...].astype(jnp.float32).T
    mixed = (key_ref[...].astype(jnp.float32) * value_ref[...].astype(jnp.float32)).astype(
        jnp.bfloat16
    )
    out_ref[...] = (
        query_ref[...].astype(jnp.float32)
        * (convolved + gain_ref[...] * mixed.astype(jnp.float32))
    ).astype(out_ref.dtype)


def finish(returned, query, key_in, value_in, skip_gain):
    return pl.pallas_call(
        finish_kernel,
        out_shape=jax.ShapeDtypeStruct(query.shape, jnp.bfloat16),
    )(returned, query, key_in, value_in, skip_gain.reshape(1, -1))


def complex_table(cos_part, sin_part, direction):
    return jnp.concatenate(
        [
            jnp.concatenate([cos_part, direction * sin_part], axis=1),
            jnp.concatenate([-direction * sin_part, cos_part], axis=1),
        ],
        axis=0,
    )


def convolve_block(got, n_dev, row_count):
    own_width = got.shape[2]
    size_a = 2 * n_dev
    kept = n_dev + 1
    padded = size_a * row_count
    stacked = got.reshape(n_dev, 2 * own_width, row_count).astype(jnp.float32)
    first_cos, first_sin = dft_table(kept, n_dev, size_a)
    first = contract("kn,ncb->kcb", jnp.concatenate([first_cos, -first_sin], axis=0), stacked)
    twiddle = angles_of(
        jnp.arange(kept, dtype=jnp.int32)[:, None]
        * jnp.arange(row_count, dtype=jnp.int32)[None, :],
        padded,
    )[:, None, :]
    real_part, imag_part = rotate(first[:kept], first[kept:], twiddle, -1)
    second_cos, second_sin = dft_table(row_count, row_count, row_count)
    prod = contract(
        "kcb,bq->kcq",
        jnp.concatenate([real_part, imag_part], axis=2),
        complex_table(second_cos, second_sin, -1),
    )
    data_real = prod[:, :own_width, :row_count]
    data_imag = prod[:, :own_width, row_count:]
    filter_real = prod[:, own_width:, :row_count]
    filter_imag = prod[:, own_width:, row_count:]
    spec_real = data_real * filter_real - data_imag * filter_imag
    spec_imag = data_real * filter_imag + data_imag * filter_real
    prod = contract(
        "kcq,qb->kcb",
        jnp.concatenate([spec_real, spec_imag], axis=2),
        complex_table(second_cos, second_sin, 1),
    )
    real_part, imag_part = rotate(prod[:, :, :row_count], prod[:, :, row_count:], twiddle, 1)
    back_cos, back_sin = dft_table(n_dev, kept, size_a)
    index = jnp.arange(kept)
    weight = jnp.where((index == 0) | (index == n_dev), 1.0, 2.0).astype(jnp.float32)[None, :]
    outcome = contract(
        "nk,kcb->ncb",
        jnp.concatenate([back_cos * weight, -back_sin * weight], axis=1),
        jnp.concatenate([real_part, imag_part], axis=0),
    )
    return (outcome * (1.0 / padded)).astype(jnp.bfloat16)


def by_channels(mixed, key_in, value_in, filters, group_index):
    n_dev = lax.axis_size("outer") * lax.axis_size("inner")
    row_count = mixed.shape[0]
    channels = mixed.shape[1]
    own_width = channels // n_dev
    pieces = 1
    piece_width = own_width // pieces
    if piece_width % 16 == 0:
        sent = prepare(key_in, value_in, filters, group_index, n_dev, pieces)
    else:
        chan_filters = select_filters(filters, group_index)
        sent = jnp.stack([mixed.T, chan_filters], axis=0).reshape(
            2, n_dev, pieces, piece_width, row_count
        )
        sent = sent.transpose(2, 1, 0, 3, 4)
    arrived = [
        lax.all_to_all(sent[piece], ("outer", "inner"), split_axis=0, concat_axis=0, tiled=True)
        for piece in range(pieces)
    ]
    results = []
    outcome = None
    for piece in range(pieces):
        got = arrived[piece]
        if outcome is not None:
            outcome, got = lax.optimization_barrier((outcome, got))
        outcome = convolve_block(got, n_dev, row_count)
        results.append(outcome)
    returned = lax.all_to_all(
        jnp.stack(results, axis=1), ("outer", "inner"), split_axis=0, concat_axis=0, tiled=True
    )
    return returned.reshape(channels, row_count)


def on_device(query, key_in, value_in, filters, group_index, skip_gain):
    mixed = (key_in.astype(jnp.float32) * value_in.astype(jnp.float32)).astype(jnp.bfloat16)
    convolved = by_channels(mixed, key_in, value_in, filters, group_index).T.astype(jnp.float32)
    mixed_wide = mixed.astype(jnp.float32)
    return (query.astype(jnp.float32) * (convolved + skip_gain[None, :] * mixed_wide)).astype(
        jnp.bfloat16
    )


def solution(mesh):
    placed = (
        P(("outer", "inner"), None),
        P(("outer", "inner"), None),
        P(("outer", "inner"), None),
        P(("outer", "inner"), None),
        P(),
        P(),
    )
    return jax.shard_map(
        on_device,
        mesh=mesh,
        in_specs=placed,
        out_specs=P(("outer", "inner"), None),
        check_vma=False,
    )
```

```python
import math

import jax
import jax.numpy as jnp
from jax import lax
from jax.sharding import PartitionSpec as P
from jax.experimental import pallas as pl


def contract(pattern, left_op, right_op):
    return jnp.einsum(
        pattern,
        left_op,
        right_op,
        precision=lax.Precision.HIGH,
        preferred_element_type=jnp.float32,
    )


def angles_of(numerator, period):
    return 2.0 * math.pi / period * jnp.mod(numerator, period).astype(jnp.float32)


def dft_table(count_out, count_in, period):
    index_grid = (
        jnp.arange(count_out, dtype=jnp.int32)[:, None]
        * jnp.arange(count_in, dtype=jnp.int32)[None, :]
    )
    phases = angles_of(index_grid, period)
    return (jnp.cos(phases), jnp.sin(phases))


def rotate(real_part, imag_part, phases, direction):
    cosine = jnp.cos(phases)
    sine_part = jnp.sin(phases)
    if direction < 0:
        return (
            real_part * cosine + imag_part * sine_part,
            imag_part * cosine - real_part * sine_part,
        )
    return (real_part * cosine - imag_part * sine_part, imag_part * cosine + real_part * sine_part)


def transform(pattern, table_cos, table_sin, real_part, imag_part, direction):
    out_real = contract(pattern, table_cos, real_part) - direction * contract(
        pattern, table_sin, imag_part
    )
    out_imag = contract(pattern, table_cos, imag_part) + direction * contract(
        pattern, table_sin, real_part
    )
    return (out_real, out_imag)


def select_kernel(index_ref, filters_ref, out_ref):
    index = index_ref[...]
    groups = filters_ref.shape[1]
    onehot = (
        index == lax.broadcasted_iota(jnp.int32, (index.shape[0], groups), 1)
    ).astype(jnp.bfloat16)
    out_ref[...] = lax.dot_general(
        onehot,
        filters_ref[...],
        (((1,), (1,)), ((), ())),
        preferred_element_type=jnp.float32,
    ).astype(out_ref.dtype)


def select_filters(filters, group_index):
    channels = group_index.shape[0]
    return pl.pallas_call(
        select_kernel,
        out_shape=jax.ShapeDtypeStruct((channels, filters.shape[0]), jnp.bfloat16),
    )(group_index.reshape(channels, 1), filters)


def prep_kernel(key_ref, value_ref, filters_ref, index_ref, *out_refs):
    pieces = len(out_refs)
    n_dev, _, piece_width, _ = out_refs[0].shape
    mixed = (key_ref[...].astype(jnp.float32) * value_ref[...].astype(jnp.float32)).astype(
        jnp.bfloat16
    )
    mixed_t = mixed.astype(jnp.float32).T
    groups = filters_ref.shape[1]
    channels = index_ref.shape[1]
    onehot_t = (
        lax.broadcasted_iota(jnp.int32, (groups, channels), 0) == index_ref[...]
    ).astype(jnp.bfloat16)
    picked = jnp.dot(filters_ref[...], onehot_t, preferred_element_type=jnp.float32).T
    for dest in range(n_dev):
        for piece in range(pieces):
            low = (dest * pieces + piece) * piece_width
            out_refs[piece][dest, 0] = mixed_t[low : low + piece_width].astype(jnp.bfloat16)
            out_refs[piece][dest, 1] = picked[low : low + piece_width].astype(jnp.bfloat16)


def prepare(key_in, value_in, filters, group_index, n_dev, pieces):
    row_count, channels = key_in.shape
    piece_width = channels // (n_dev * pieces)
    return pl.pallas_call(
        prep_kernel,
        out_shape=tuple(
            jax.ShapeDtypeStruct((n_dev, 2, piece_width, row_count), jnp.bfloat16)
            for _ in range(pieces)
        ),
    )(key_in, value_in, filters, group_index.reshape(1, channels))


def finish_kernel(returned_ref, query_ref, key_ref, value_ref, gain_ref, out_ref):
    convolved = returned_ref[...].astype(jnp.float32).T
    mixed = (key_ref[...].astype(jnp.float32) * value_ref[...].astype(jnp.float32)).astype(
        jnp.bfloat16
    )
    out_ref[...] = (
        query_ref[...].astype(jnp.float32)
        * (convolved + gain_ref[...] * mixed.astype(jnp.float32))
    ).astype(out_ref.dtype)


def finish(returned, query, key_in, value_in, skip_gain):
    return pl.pallas_call(
        finish_kernel,
        out_shape=jax.ShapeDtypeStruct(query.shape, jnp.bfloat16),
    )(returned, query, key_in, value_in, skip_gain.reshape(1, -1))


def complex_table(cos_part, sin_part, direction):
    return jnp.concatenate(
        [
            jnp.concatenate([cos_part, direction * sin_part], axis=1),
            jnp.concatenate([-direction * sin_part, cos_part], axis=1),
        ],
        axis=0,
    )


def convolve_block(got, n_dev, row_count, order):
    own_width = got.shape[2]
    size_a = 2 * n_dev
    kept = n_dev + 1
    padded = size_a * row_count
    stacked = got.reshape(n_dev, 2 * own_width, row_count).astype(jnp.float32)
    first_cos, first_sin = dft_table(kept, n_dev, size_a)
    first = contract(
        "kn,ncb->kcb", jnp.concatenate([first_cos, -first_sin], axis=0)[:, order], stacked
    )
    twiddle = angles_of(
        jnp.arange(kept, dtype=jnp.int32)[:, None]
        * jnp.arange(row_count, dtype=jnp.int32)[None, :],
        padded,
    )[:, None, :]
    real_part, imag_part = rotate(first[:kept], first[kept:], twiddle, -1)
    second_cos, second_sin = dft_table(row_count, row_count, row_count)
    prod = contract(
        "kcb,bq->kcq",
        jnp.concatenate([real_part, imag_part], axis=2),
        complex_table(second_cos, second_sin, -1),
    )
    data_real = prod[:, :own_width, :row_count]
    data_imag = prod[:, :own_width, row_count:]
    filter_real = prod[:, own_width:, :row_count]
    filter_imag = prod[:, own_width:, row_count:]
    spec_real = data_real * filter_real - data_imag * filter_imag
    spec_imag = data_real * filter_imag + data_imag * filter_real
    prod = contract(
        "kcq,qb->kcb",
        jnp.concatenate([spec_real, spec_imag], axis=2),
        complex_table(second_cos, second_sin, 1),
    )
    real_part, imag_part = rotate(prod[:, :, :row_count], prod[:, :, row_count:], twiddle, 1)
    back_cos, back_sin = dft_table(n_dev, kept, size_a)
    index = jnp.arange(kept)
    weight = jnp.where((index == 0) | (index == n_dev), 1.0, 2.0).astype(jnp.float32)[None, :]
    outcome = contract(
        "nk,kcb->ncb",
        jnp.concatenate([back_cos * weight, -back_sin * weight], axis=1)[order],
        jnp.concatenate([real_part, imag_part], axis=0),
    )
    return (outcome * (1.0 / padded)).astype(jnp.bfloat16)


def by_channels(mixed, key_in, value_in, filters, group_index):
    n_dev = lax.axis_size("outer") * lax.axis_size("inner")
    row_count = mixed.shape[0]
    channels = mixed.shape[1]
    own_width = channels // n_dev
    pieces = 1
    piece_width = own_width // pieces
    if piece_width % 16 == 0:
        sent = prepare(key_in, value_in, filters, group_index, n_dev, pieces)
    else:
        chan_filters = select_filters(filters, group_index)
        sent = jnp.stack([mixed.T, chan_filters], axis=0).reshape(
            2, n_dev, pieces, piece_width, row_count
        )
        sent = sent.transpose(2, 1, 0, 3, 4)
    axes = ("inner", "outer")
    order = jnp.arange(n_dev).reshape(lax.axis_size("outer"), lax.axis_size("inner")).T.reshape(-1)
    arrived = [
        lax.all_to_all(sent[piece], axes, split_axis=0, concat_axis=0, tiled=True)
        for piece in range(pieces)
    ]
    results = []
    outcome = None
    for piece in range(pieces):
        got = arrived[piece]
        if outcome is not None:
            outcome, got = lax.optimization_barrier((outcome, got))
        outcome = convolve_block(got, n_dev, row_count, order)
        results.append(outcome)
    returned = lax.all_to_all(
        jnp.stack(results, axis=1), axes, split_axis=0, concat_axis=0, tiled=True
    )
    return returned.reshape(channels, row_count)


def on_device(query, key_in, value_in, filters, group_index, skip_gain):
    mixed = (key_in.astype(jnp.float32) * value_in.astype(jnp.float32)).astype(jnp.bfloat16)
    convolved = by_channels(mixed, key_in, value_in, filters, group_index).T.astype(jnp.float32)
    mixed_wide = mixed.astype(jnp.float32)
    return (query.astype(jnp.float32) * (convolved + skip_gain[None, :] * mixed_wide)).astype(
        jnp.bfloat16
    )


def solution(mesh):
    placed = (
        P(("outer", "inner"), None),
        P(("outer", "inner"), None),
        P(("outer", "inner"), None),
        P(("outer", "inner"), None),
        P(),
        P(),
    )
    return jax.shard_map(
        on_device,
        mesh=mesh,
        in_specs=placed,
        out_specs=P(("outer", "inner"), None),
        check_vma=False,
    )
```

```python
import math

import jax
import jax.numpy as jnp
from jax import lax
from jax.sharding import PartitionSpec as P
from jax.experimental import pallas as pl


def contract(pattern, left_op, right_op):
    return jnp.einsum(
        pattern,
        left_op,
        right_op,
        precision=lax.Precision.HIGH,
        preferred_element_type=jnp.float32,
    )


def angles_of(numerator, period):
    return 2.0 * math.pi / period * jnp.mod(numerator, period).astype(jnp.float32)


def dft_table(count_out, count_in, period):
    index_grid = (
        jnp.arange(count_out, dtype=jnp.int32)[:, None]
        * jnp.arange(count_in, dtype=jnp.int32)[None, :]
    )
    phases = angles_of(index_grid, period)
    return (jnp.cos(phases), jnp.sin(phases))


def rotate(real_part, imag_part, phases, direction):
    cosine = jnp.cos(phases)
    sine_part = jnp.sin(phases)
    if direction < 0:
        return (
            real_part * cosine + imag_part * sine_part,
            imag_part * cosine - real_part * sine_part,
        )
    return (real_part * cosine - imag_part * sine_part, imag_part * cosine + real_part * sine_part)


def transform(pattern, table_cos, table_sin, real_part, imag_part, direction):
    out_real = contract(pattern, table_cos, real_part) - direction * contract(
        pattern, table_sin, imag_part
    )
    out_imag = contract(pattern, table_cos, imag_part) + direction * contract(
        pattern, table_sin, real_part
    )
    return (out_real, out_imag)


def select_kernel(index_ref, filters_ref, out_ref):
    index = index_ref[...]
    groups = filters_ref.shape[1]
    onehot = (
        index == lax.broadcasted_iota(jnp.int32, (index.shape[0], groups), 1)
    ).astype(jnp.bfloat16)
    out_ref[...] = lax.dot_general(
        onehot,
        filters_ref[...],
        (((1,), (1,)), ((), ())),
        preferred_element_type=jnp.float32,
    ).astype(out_ref.dtype)


def select_filters(filters, group_index):
    channels = group_index.shape[0]
    return pl.pallas_call(
        select_kernel,
        out_shape=jax.ShapeDtypeStruct((channels, filters.shape[0]), jnp.bfloat16),
    )(group_index.reshape(channels, 1), filters)


def prep_kernel(key_ref, value_ref, filters_ref, index_ref, *out_refs):
    pieces = len(out_refs)
    n_dev, _, piece_width, _ = out_refs[0].shape
    mixed = (key_ref[...].astype(jnp.float32) * value_ref[...].astype(jnp.float32)).astype(
        jnp.bfloat16
    )
    mixed_t = mixed.astype(jnp.float32).T
    groups = filters_ref.shape[1]
    channels = index_ref.shape[1]
    onehot_t = (
        lax.broadcasted_iota(jnp.int32, (groups, channels), 0) == index_ref[...]
    ).astype(jnp.bfloat16)
    picked = jnp.dot(filters_ref[...], onehot_t, preferred_element_type=jnp.float32).T
    for dest in range(n_dev):
        for piece in range(pieces):
            low = (dest * pieces + piece) * piece_width
            out_refs[piece][dest, 0] = mixed_t[low : low + piece_width].astype(jnp.bfloat16)
            out_refs[piece][dest, 1] = picked[low : low + piece_width].astype(jnp.bfloat16)


def prepare(key_in, value_in, filters, group_index, n_dev, pieces):
    row_count, channels = key_in.shape
    piece_width = channels // (n_dev * pieces)
    return pl.pallas_call(
        prep_kernel,
        out_shape=tuple(
            jax.ShapeDtypeStruct((n_dev, 2, piece_width, row_count), jnp.bfloat16)
            for _ in range(pieces)
        ),
    )(key_in, value_in, filters, group_index.reshape(1, channels))


def finish_kernel(returned_ref, query_ref, key_ref, value_ref, gain_ref, out_ref):
    convolved = returned_ref[...].astype(jnp.float32).T
    mixed = (key_ref[...].astype(jnp.float32) * value_ref[...].astype(jnp.float32)).astype(
        jnp.bfloat16
    )
    out_ref[...] = (
        query_ref[...].astype(jnp.float32)
        * (convolved + gain_ref[...] * mixed.astype(jnp.float32))
    ).astype(out_ref.dtype)


def finish(returned, query, key_in, value_in, skip_gain):
    return pl.pallas_call(
        finish_kernel,
        out_shape=jax.ShapeDtypeStruct(query.shape, jnp.bfloat16),
    )(returned, query, key_in, value_in, skip_gain.reshape(1, -1))


def complex_table(cos_part, sin_part, direction):
    return jnp.concatenate(
        [
            jnp.concatenate([cos_part, direction * sin_part], axis=1),
            jnp.concatenate([-direction * sin_part, cos_part], axis=1),
        ],
        axis=0,
    )


def convolve_block(got, n_dev, row_count):
    own_width = got.shape[2]
    size_a = 2 * n_dev
    kept = n_dev + 1
    padded = size_a * row_count
    stacked = got.reshape(n_dev, 2 * own_width, row_count)
    first_cos, first_sin = dft_table(kept, n_dev, size_a)
    first_table = jnp.concatenate([first_cos, -first_sin], axis=0)
    table_high = first_table.astype(jnp.bfloat16)
    table_low = (first_table - table_high.astype(jnp.float32)).astype(jnp.bfloat16)
    first = jnp.einsum(
        "kn,ncb->kcb",
        jnp.concatenate([table_high, table_low], axis=1),
        jnp.concatenate([stacked, stacked], axis=0),
        preferred_element_type=jnp.float32,
    )
    twiddle = angles_of(
        jnp.arange(kept, dtype=jnp.int32)[:, None]
        * jnp.arange(row_count, dtype=jnp.int32)[None, :],
        padded,
    )[:, None, :]
    real_part, imag_part = rotate(first[:kept], first[kept:], twiddle, -1)
    second_cos, second_sin = dft_table(row_count, row_count, row_count)
    prod = contract(
        "kcb,bq->kcq",
        jnp.concatenate([real_part, imag_part], axis=2),
        complex_table(second_cos, second_sin, -1),
    )
    data_real = prod[:, :own_width, :row_count]
    data_imag = prod[:, :own_width, row_count:]
    filter_real = prod[:, own_width:, :row_count]
    filter_imag = prod[:, own_width:, row_count:]
    spec_real = data_real * filter_real - data_imag * filter_imag
    spec_imag = data_real * filter_imag + data_imag * filter_real
    prod = contract(
        "kcq,qb->kcb",
        jnp.concatenate([spec_real, spec_imag], axis=2),
        complex_table(second_cos, second_sin, 1),
    )
    real_part, imag_part = rotate(prod[:, :, :row_count], prod[:, :, row_count:], twiddle, 1)
    back_cos, back_sin = dft_table(n_dev, kept, size_a)
    index = jnp.arange(kept)
    weight = jnp.where((index == 0) | (index == n_dev), 1.0, 2.0).astype(jnp.float32)[None, :]
    outcome = contract(
        "nk,kcb->ncb",
        jnp.concatenate([back_cos * weight, -back_sin * weight], axis=1),
        jnp.concatenate([real_part, imag_part], axis=0),
    )
    return (outcome * (1.0 / padded)).astype(jnp.bfloat16)


def by_channels(mixed, key_in, value_in, filters, group_index):
    n_dev = lax.axis_size("outer") * lax.axis_size("inner")
    row_count = mixed.shape[0]
    channels = mixed.shape[1]
    own_width = channels // n_dev
    pieces = 1
    piece_width = own_width // pieces
    if piece_width % 16 == 0:
        sent = prepare(key_in, value_in, filters, group_index, n_dev, pieces)
    else:
        chan_filters = select_filters(filters, group_index)
        sent = jnp.stack([mixed.T, chan_filters], axis=0).reshape(
            2, n_dev, pieces, piece_width, row_count
        )
        sent = sent.transpose(2, 1, 0, 3, 4)
    arrived = [
        lax.all_to_all(sent[piece], ("outer", "inner"), split_axis=0, concat_axis=0, tiled=True)
        for piece in range(pieces)
    ]
    results = []
    outcome = None
    for piece in range(pieces):
        got = arrived[piece]
        if outcome is not None:
            outcome, got = lax.optimization_barrier((outcome, got))
        outcome = convolve_block(got, n_dev, row_count)
        results.append(outcome)
    returned = lax.all_to_all(
        jnp.stack(results, axis=1), ("outer", "inner"), split_axis=0, concat_axis=0, tiled=True
    )
    return returned.reshape(channels, row_count)


def on_device(query, key_in, value_in, filters, group_index, skip_gain):
    mixed = (key_in.astype(jnp.float32) * value_in.astype(jnp.float32)).astype(jnp.bfloat16)
    convolved = by_channels(mixed, key_in, value_in, filters, group_index).T.astype(jnp.float32)
    mixed_wide = mixed.astype(jnp.float32)
    return (query.astype(jnp.float32) * (convolved + skip_gain[None, :] * mixed_wide)).astype(
        jnp.bfloat16
    )


def solution(mesh):
    placed = (
        P(("outer", "inner"), None),
        P(("outer", "inner"), None),
        P(("outer", "inner"), None),
        P(("outer", "inner"), None),
        P(),
        P(),
    )
    return jax.shard_map(
        on_device,
        mesh=mesh,
        in_specs=placed,
        out_specs=P(("outer", "inner"), None),
        check_vma=False,
    )
```

```python
import math

import jax
import jax.numpy as jnp
from jax import lax
from jax.sharding import PartitionSpec as P
from jax.experimental import pallas as pl


def contract(pattern, left_op, right_op):
    return jnp.einsum(
        pattern,
        left_op,
        right_op,
        precision=lax.Precision.HIGH,
        preferred_element_type=jnp.float32,
    )


def angles_of(numerator, period):
    return 2.0 * math.pi / period * jnp.mod(numerator, period).astype(jnp.float32)


def dft_table(count_out, count_in, period):
    index_grid = (
        jnp.arange(count_out, dtype=jnp.int32)[:, None]
        * jnp.arange(count_in, dtype=jnp.int32)[None, :]
    )
    phases = angles_of(index_grid, period)
    return (jnp.cos(phases), jnp.sin(phases))


def rotate(real_part, imag_part, phases, direction):
    cosine = jnp.cos(phases)
    sine_part = jnp.sin(phases)
    if direction < 0:
        return (
            real_part * cosine + imag_part * sine_part,
            imag_part * cosine - real_part * sine_part,
        )
    return (real_part * cosine - imag_part * sine_part, imag_part * cosine + real_part * sine_part)


def transform(pattern, table_cos, table_sin, real_part, imag_part, direction):
    out_real = contract(pattern, table_cos, real_part) - direction * contract(
        pattern, table_sin, imag_part
    )
    out_imag = contract(pattern, table_cos, imag_part) + direction * contract(
        pattern, table_sin, real_part
    )
    return (out_real, out_imag)


def select_kernel(index_ref, filters_ref, out_ref):
    index = index_ref[...]
    groups = filters_ref.shape[1]
    onehot = (
        index == lax.broadcasted_iota(jnp.int32, (index.shape[0], groups), 1)
    ).astype(jnp.bfloat16)
    out_ref[...] = lax.dot_general(
        onehot,
        filters_ref[...],
        (((1,), (1,)), ((), ())),
        preferred_element_type=jnp.float32,
    ).astype(out_ref.dtype)


def select_filters(filters, group_index):
    channels = group_index.shape[0]
    return pl.pallas_call(
        select_kernel,
        out_shape=jax.ShapeDtypeStruct((channels, filters.shape[0]), jnp.bfloat16),
    )(group_index.reshape(channels, 1), filters)


def prep_kernel(key_ref, value_ref, filters_ref, index_ref, *out_refs):
    pieces = len(out_refs)
    n_dev, _, piece_width, _ = out_refs[0].shape
    mixed = (key_ref[...].astype(jnp.float32) * value_ref[...].astype(jnp.float32)).astype(
        jnp.bfloat16
    )
    mixed_t = mixed.astype(jnp.float32).T
    groups = filters_ref.shape[1]
    channels = index_ref.shape[1]
    onehot_t = (
        lax.broadcasted_iota(jnp.int32, (groups, channels), 0) == index_ref[...]
    ).astype(jnp.bfloat16)
    picked = jnp.dot(filters_ref[...], onehot_t, preferred_element_type=jnp.float32).T
    for dest in range(n_dev):
        for piece in range(pieces):
            low = (dest * pieces + piece) * piece_width
            out_refs[piece][dest, 0] = mixed_t[low : low + piece_width].astype(jnp.bfloat16)
            out_refs[piece][dest, 1] = picked[low : low + piece_width].astype(jnp.bfloat16)


def prepare(key_in, value_in, filters, group_index, n_dev, pieces):
    row_count, channels = key_in.shape
    piece_width = channels // (n_dev * pieces)
    return pl.pallas_call(
        prep_kernel,
        out_shape=tuple(
            jax.ShapeDtypeStruct((n_dev, 2, piece_width, row_count), jnp.bfloat16)
            for _ in range(pieces)
        ),
    )(key_in, value_in, filters, group_index.reshape(1, channels))


def finish_kernel(returned_ref, query_ref, key_ref, value_ref, gain_ref, out_ref):
    convolved = returned_ref[...].astype(jnp.float32).T
    mixed = (key_ref[...].astype(jnp.float32) * value_ref[...].astype(jnp.float32)).astype(
        jnp.bfloat16
    )
    out_ref[...] = (
        query_ref[...].astype(jnp.float32)
        * (convolved + gain_ref[...] * mixed.astype(jnp.float32))
    ).astype(out_ref.dtype)


def finish(returned, query, key_in, value_in, skip_gain):
    return pl.pallas_call(
        finish_kernel,
        out_shape=jax.ShapeDtypeStruct(query.shape, jnp.bfloat16),
    )(returned, query, key_in, value_in, skip_gain.reshape(1, -1))


def flip_kernel(in_ref, out_ref):
    out_ref[...] = in_ref[...].astype(jnp.float32).T


def flip(block):
    return pl.pallas_call(
        flip_kernel,
        out_shape=jax.ShapeDtypeStruct((block.shape[1], block.shape[0]), jnp.float32),
    )(block)


def complex_table(cos_part, sin_part, direction):
    return jnp.concatenate(
        [
            jnp.concatenate([cos_part, direction * sin_part], axis=1),
            jnp.concatenate([-direction * sin_part, cos_part], axis=1),
        ],
        axis=0,
    )


def convolve_block(got, n_dev, row_count):
    own_width = got.shape[2]
    size_a = 2 * n_dev
    kept = n_dev + 1
    padded = size_a * row_count
    stacked = got.reshape(n_dev, 2 * own_width, row_count).astype(jnp.float32)
    first_cos, first_sin = dft_table(kept, n_dev, size_a)
    first = contract("kn,ncb->kcb", jnp.concatenate([first_cos, -first_sin], axis=0), stacked)
    twiddle = angles_of(
        jnp.arange(kept, dtype=jnp.int32)[:, None]
        * jnp.arange(row_count, dtype=jnp.int32)[None, :],
        padded,
    )[:, None, :]
    real_part, imag_part = rotate(first[:kept], first[kept:], twiddle, -1)
    second_cos, second_sin = dft_table(row_count, row_count, row_count)
    prod = contract(
        "kcb,bq->kcq",
        jnp.concatenate([real_part, imag_part], axis=2),
        complex_table(second_cos, second_sin, -1),
    )
    data_real = prod[:, :own_width, :row_count]
    data_imag = prod[:, :own_width, row_count:]
    filter_real = prod[:, own_width:, :row_count]
    filter_imag = prod[:, own_width:, row_count:]
    spec_real = data_real * filter_real - data_imag * filter_imag
    spec_imag = data_real * filter_imag + data_imag * filter_real
    prod = contract(
        "kcq,qb->kcb",
        jnp.concatenate([spec_real, spec_imag], axis=2),
        complex_table(second_cos, second_sin, 1),
    )
    real_part, imag_part = rotate(prod[:, :, :row_count], prod[:, :, row_count:], twiddle, 1)
    back_cos, back_sin = dft_table(n_dev, kept, size_a)
    index = jnp.arange(kept)
    weight = jnp.where((index == 0) | (index == n_dev), 1.0, 2.0).astype(jnp.float32)[None, :]
    outcome = contract(
        "nk,kcb->ncb",
        jnp.concatenate([back_cos * weight, -back_sin * weight], axis=1),
        jnp.concatenate([real_part, imag_part], axis=0),
    )
    return (outcome * (1.0 / padded)).astype(jnp.bfloat16)


def by_channels(mixed, key_in, value_in, filters, group_index):
    n_dev = lax.axis_size("outer") * lax.axis_size("inner")
    row_count = mixed.shape[0]
    channels = mixed.shape[1]
    own_width = channels // n_dev
    pieces = 1
    piece_width = own_width // pieces
    if piece_width % 16 == 0:
        sent = prepare(key_in, value_in, filters, group_index, n_dev, pieces)
    else:
        chan_filters = select_filters(filters, group_index)
        sent = jnp.stack([mixed.T, chan_filters], axis=0).reshape(
            2, n_dev, pieces, piece_width, row_count
        )
        sent = sent.transpose(2, 1, 0, 3, 4)
    arrived = [
        lax.all_to_all(sent[piece], ("outer", "inner"), split_axis=0, concat_axis=0, tiled=True)
        for piece in range(pieces)
    ]
    results = []
    outcome = None
    for piece in range(pieces):
        got = arrived[piece]
        if outcome is not None:
            outcome, got = lax.optimization_barrier((outcome, got))
        outcome = convolve_block(got, n_dev, row_count)
        results.append(outcome)
    returned = lax.all_to_all(
        jnp.stack(results, axis=1), ("outer", "inner"), split_axis=0, concat_axis=0, tiled=True
    )
    return returned.reshape(channels, row_count)


def on_device(query, key_in, value_in, filters, group_index, skip_gain):
    mixed = (key_in.astype(jnp.float32) * value_in.astype(jnp.float32)).astype(jnp.bfloat16)
    convolved = flip(by_channels(mixed, key_in, value_in, filters, group_index))
    mixed_wide = mixed.astype(jnp.float32)
    return (query.astype(jnp.float32) * (convolved + skip_gain[None, :] * mixed_wide)).astype(
        jnp.bfloat16
    )


def solution(mesh):
    placed = (
        P(("outer", "inner"), None),
        P(("outer", "inner"), None),
        P(("outer", "inner"), None),
        P(("outer", "inner"), None),
        P(),
        P(),
    )
    return jax.shard_map(
        on_device,
        mesh=mesh,
        in_specs=placed,
        out_specs=P(("outer", "inner"), None),
        check_vma=False,
    )
```

```python
import math

import jax
import jax.numpy as jnp
from jax import lax
from jax.sharding import PartitionSpec as P
from jax.experimental import pallas as pl


def contract(pattern, left_op, right_op):
    return jnp.einsum(
        pattern,
        left_op,
        right_op,
        precision=lax.Precision.HIGH,
        preferred_element_type=jnp.float32,
    )


def angles_of(numerator, period):
    return 2.0 * math.pi / period * jnp.mod(numerator, period).astype(jnp.float32)


def dft_table(count_out, count_in, period):
    index_grid = (
        jnp.arange(count_out, dtype=jnp.int32)[:, None]
        * jnp.arange(count_in, dtype=jnp.int32)[None, :]
    )
    phases = angles_of(index_grid, period)
    return (jnp.cos(phases), jnp.sin(phases))


def rotate(real_part, imag_part, phases, direction):
    cosine = jnp.cos(phases)
    sine_part = jnp.sin(phases)
    if direction < 0:
        return (
            real_part * cosine + imag_part * sine_part,
            imag_part * cosine - real_part * sine_part,
        )
    return (real_part * cosine - imag_part * sine_part, imag_part * cosine + real_part * sine_part)


def transform(pattern, table_cos, table_sin, real_part, imag_part, direction):
    out_real = contract(pattern, table_cos, real_part) - direction * contract(
        pattern, table_sin, imag_part
    )
    out_imag = contract(pattern, table_cos, imag_part) + direction * contract(
        pattern, table_sin, real_part
    )
    return (out_real, out_imag)


def select_kernel(index_ref, filters_ref, out_ref):
    index = index_ref[...]
    groups = filters_ref.shape[1]
    onehot = (
        index == lax.broadcasted_iota(jnp.int32, (index.shape[0], groups), 1)
    ).astype(jnp.bfloat16)
    out_ref[...] = lax.dot_general(
        onehot,
        filters_ref[...],
        (((1,), (1,)), ((), ())),
        preferred_element_type=jnp.float32,
    ).astype(out_ref.dtype)


def select_filters(filters, group_index):
    channels = group_index.shape[0]
    return pl.pallas_call(
        select_kernel,
        out_shape=jax.ShapeDtypeStruct((channels, filters.shape[0]), jnp.bfloat16),
    )(group_index.reshape(channels, 1), filters)


def prep_kernel(key_ref, value_ref, filters_ref, index_ref, *out_refs):
    pieces = len(out_refs)
    n_dev, _, piece_width, _ = out_refs[0].shape
    mixed = (key_ref[...].astype(jnp.float32) * value_ref[...].astype(jnp.float32)).astype(
        jnp.bfloat16
    )
    mixed_t = mixed.T
    groups = filters_ref.shape[1]
    channels = index_ref.shape[1]
    onehot_t = (
        lax.broadcasted_iota(jnp.int32, (groups, channels), 0) == index_ref[...]
    ).astype(jnp.bfloat16)
    picked = jnp.dot(filters_ref[...], onehot_t, preferred_element_type=jnp.float32).astype(
        jnp.bfloat16
    ).T
    for dest in range(n_dev):
        for piece in range(pieces):
            low = (dest * pieces + piece) * piece_width
            out_refs[piece][dest, 0] = mixed_t[low : low + piece_width].astype(jnp.bfloat16)
            out_refs[piece][dest, 1] = picked[low : low + piece_width].astype(jnp.bfloat16)


def prepare(key_in, value_in, filters, group_index, n_dev, pieces):
    row_count, channels = key_in.shape
    piece_width = channels // (n_dev * pieces)
    return pl.pallas_call(
        prep_kernel,
        out_shape=tuple(
            jax.ShapeDtypeStruct((n_dev, 2, piece_width, row_count), jnp.bfloat16)
            for _ in range(pieces)
        ),
    )(key_in, value_in, filters, group_index.reshape(1, channels))


def finish_kernel(returned_ref, query_ref, key_ref, value_ref, gain_ref, out_ref):
    convolved = returned_ref[...].astype(jnp.float32).T
    mixed = (key_ref[...].astype(jnp.float32) * value_ref[...].astype(jnp.float32)).astype(
        jnp.bfloat16
    )
    out_ref[...] = (
        query_ref[...].astype(jnp.float32)
        * (convolved + gain_ref[...] * mixed.astype(jnp.float32))
    ).astype(out_ref.dtype)


def finish(returned, query, key_in, value_in, skip_gain):
    return pl.pallas_call(
        finish_kernel,
        out_shape=jax.ShapeDtypeStruct(query.shape, jnp.bfloat16),
    )(returned, query, key_in, value_in, skip_gain.reshape(1, -1))


def complex_table(cos_part, sin_part, direction):
    return jnp.concatenate(
        [
            jnp.concatenate([cos_part, direction * sin_part], axis=1),
            jnp.concatenate([-direction * sin_part, cos_part], axis=1),
        ],
        axis=0,
    )


def convolve_block(got, n_dev, row_count):
    own_width = got.shape[2]
    size_a = 2 * n_dev
    kept = n_dev + 1
    padded = size_a * row_count
    stacked = got.reshape(n_dev, 2 * own_width, row_count).astype(jnp.float32)
    first_cos, first_sin = dft_table(kept, n_dev, size_a)
    first = contract("kn,ncb->kcb", jnp.concatenate([first_cos, -first_sin], axis=0), stacked)
    twiddle = angles_of(
        jnp.arange(kept, dtype=jnp.int32)[:, None]
        * jnp.arange(row_count, dtype=jnp.int32)[None, :],
        padded,
    )[:, None, :]
    real_part, imag_part = rotate(first[:kept], first[kept:], twiddle, -1)
    second_cos, second_sin = dft_table(row_count, row_count, row_count)
    prod = contract(
        "kcb,bq->kcq",
        jnp.concatenate([real_part, imag_part], axis=2),
        complex_table(second_cos, second_sin, -1),
    )
    data_real = prod[:, :own_width, :row_count]
    data_imag = prod[:, :own_width, row_count:]
    filter_real = prod[:, own_width:, :row_count]
    filter_imag = prod[:, own_width:, row_count:]
    spec_real = data_real * filter_real - data_imag * filter_imag
    spec_imag = data_real * filter_imag + data_imag * filter_real
    prod = contract(
        "kcq,qb->kcb",
        jnp.concatenate([spec_real, spec_imag], axis=2),
        complex_table(second_cos, second_sin, 1),
    )
    real_part, imag_part = rotate(prod[:, :, :row_count], prod[:, :, row_count:], twiddle, 1)
    back_cos, back_sin = dft_table(n_dev, kept, size_a)
    index = jnp.arange(kept)
    weight = jnp.where((index == 0) | (index == n_dev), 1.0, 2.0).astype(jnp.float32)[None, :]
    outcome = contract(
        "nk,kcb->ncb",
        jnp.concatenate([back_cos * weight, -back_sin * weight], axis=1),
        jnp.concatenate([real_part, imag_part], axis=0),
    )
    return (outcome * (1.0 / padded)).astype(jnp.bfloat16)


def by_channels(mixed, key_in, value_in, filters, group_index):
    n_dev = lax.axis_size("outer") * lax.axis_size("inner")
    row_count = mixed.shape[0]
    channels = mixed.shape[1]
    own_width = channels // n_dev
    pieces = 1
    piece_width = own_width // pieces
    if piece_width % 16 == 0:
        sent = prepare(key_in, value_in, filters, group_index, n_dev, pieces)
    else:
        chan_filters = select_filters(filters, group_index)
        sent = jnp.stack([mixed.T, chan_filters], axis=0).reshape(
            2, n_dev, pieces, piece_width, row_count
        )
        sent = sent.transpose(2, 1, 0, 3, 4)
    arrived = [
        lax.all_to_all(sent[piece], ("outer", "inner"), split_axis=0, concat_axis=0, tiled=True)
        for piece in range(pieces)
    ]
    results = []
    outcome = None
    for piece in range(pieces):
        got = arrived[piece]
        if outcome is not None:
            outcome, got = lax.optimization_barrier((outcome, got))
        outcome = convolve_block(got, n_dev, row_count)
        results.append(outcome)
    returned = lax.all_to_all(
        jnp.stack(results, axis=1), ("outer", "inner"), split_axis=0, concat_axis=0, tiled=True
    )
    return returned.reshape(channels, row_count)


def on_device(query, key_in, value_in, filters, group_index, skip_gain):
    mixed = (key_in.astype(jnp.float32) * value_in.astype(jnp.float32)).astype(jnp.bfloat16)
    convolved = by_channels(mixed, key_in, value_in, filters, group_index).T.astype(jnp.float32)
    mixed_wide = mixed.astype(jnp.float32)
    return (query.astype(jnp.float32) * (convolved + skip_gain[None, :] * mixed_wide)).astype(
        jnp.bfloat16
    )


def solution(mesh):
    placed = (
        P(("outer", "inner"), None),
        P(("outer", "inner"), None),
        P(("outer", "inner"), None),
        P(("outer", "inner"), None),
        P(),
        P(),
    )
    return jax.shard_map(
        on_device,
        mesh=mesh,
        in_specs=placed,
        out_specs=P(("outer", "inner"), None),
        check_vma=False,
    )
```

```python
import math

import jax
import jax.numpy as jnp
from jax import lax
from jax.sharding import PartitionSpec as P
from jax.experimental import pallas as pl


def contract(pattern, left_op, right_op):
    return jnp.einsum(
        pattern,
        left_op,
        right_op,
        precision=lax.Precision.HIGH,
        preferred_element_type=jnp.float32,
    )


def angles_of(numerator, period):
    return 2.0 * math.pi / period * jnp.mod(numerator, period).astype(jnp.float32)


def dft_table(count_out, count_in, period):
    index_grid = (
        jnp.arange(count_out, dtype=jnp.int32)[:, None]
        * jnp.arange(count_in, dtype=jnp.int32)[None, :]
    )
    phases = angles_of(index_grid, period)
    return (jnp.cos(phases), jnp.sin(phases))


def rotate(real_part, imag_part, phases, direction):
    cosine = jnp.cos(phases)
    sine_part = jnp.sin(phases)
    if direction < 0:
        return (
            real_part * cosine + imag_part * sine_part,
            imag_part * cosine - real_part * sine_part,
        )
    return (real_part * cosine - imag_part * sine_part, imag_part * cosine + real_part * sine_part)


def transform(pattern, table_cos, table_sin, real_part, imag_part, direction):
    out_real = contract(pattern, table_cos, real_part) - direction * contract(
        pattern, table_sin, imag_part
    )
    out_imag = contract(pattern, table_cos, imag_part) + direction * contract(
        pattern, table_sin, real_part
    )
    return (out_real, out_imag)


def select_kernel(index_ref, filters_ref, out_ref):
    index = index_ref[...]
    groups = filters_ref.shape[1]
    onehot = (
        index == lax.broadcasted_iota(jnp.int32, (index.shape[0], groups), 1)
    ).astype(jnp.bfloat16)
    out_ref[...] = lax.dot_general(
        onehot,
        filters_ref[...],
        (((1,), (1,)), ((), ())),
        preferred_element_type=jnp.float32,
    ).astype(out_ref.dtype)


def select_filters(filters, group_index):
    channels = group_index.shape[0]
    return pl.pallas_call(
        select_kernel,
        out_shape=jax.ShapeDtypeStruct((channels, filters.shape[0]), jnp.bfloat16),
    )(group_index.reshape(channels, 1), filters)


def prep_kernel(key_ref, value_ref, filters_ref, index_ref, *out_refs):
    pieces = len(out_refs)
    n_dev, _, piece_width, _ = out_refs[0].shape
    mixed = (key_ref[...].astype(jnp.float32) * value_ref[...].astype(jnp.float32)).astype(
        jnp.bfloat16
    )
    mixed_t = mixed.astype(jnp.float32).T
    groups = filters_ref.shape[1]
    channels = index_ref.shape[1]
    onehot_t = (
        lax.broadcasted_iota(jnp.int32, (groups, channels), 0) == index_ref[...]
    ).astype(jnp.bfloat16)
    picked = jnp.dot(filters_ref[...], onehot_t, preferred_element_type=jnp.float32).T
    for dest in range(n_dev):
        for piece in range(pieces):
            low = (dest * pieces + piece) * piece_width
            out_refs[piece][dest, 0] = mixed_t[low : low + piece_width].astype(jnp.bfloat16)
            out_refs[piece][dest, 1] = picked[low : low + piece_width].astype(jnp.bfloat16)


def prepare(key_in, value_in, filters, group_index, n_dev, pieces):
    row_count, channels = key_in.shape
    piece_width = channels // (n_dev * pieces)
    return pl.pallas_call(
        prep_kernel,
        out_shape=tuple(
            jax.ShapeDtypeStruct((n_dev, 2, piece_width, row_count), jnp.bfloat16)
            for _ in range(pieces)
        ),
    )(key_in, value_in, filters, group_index.reshape(1, channels))


def finish_kernel(returned_ref, query_ref, key_ref, value_ref, gain_ref, out_ref):
    convolved = returned_ref[...].astype(jnp.float32).T
    mixed = (key_ref[...].astype(jnp.float32) * value_ref[...].astype(jnp.float32)).astype(
        jnp.bfloat16
    )
    out_ref[...] = (
        query_ref[...].astype(jnp.float32)
        * (convolved + gain_ref[...] * mixed.astype(jnp.float32))
    ).astype(out_ref.dtype)


def finish(returned, query, key_in, value_in, skip_gain):
    return pl.pallas_call(
        finish_kernel,
        out_shape=jax.ShapeDtypeStruct(query.shape, jnp.bfloat16),
    )(returned, query, key_in, value_in, skip_gain.reshape(1, -1))


def complex_table(cos_part, sin_part, direction):
    return jnp.concatenate(
        [
            jnp.concatenate([cos_part, direction * sin_part], axis=1),
            jnp.concatenate([-direction * sin_part, cos_part], axis=1),
        ],
        axis=0,
    )


def convolve_block(got, n_dev, row_count):
    own_width = got.shape[2]
    size_a = 2 * n_dev
    kept = n_dev + 1
    padded = size_a * row_count
    stacked = got.reshape(n_dev, 2 * own_width, row_count).astype(jnp.float32)
    first_cos, first_sin = dft_table(kept, n_dev, size_a)
    first = contract("kn,ncb->kcb", jnp.concatenate([first_cos, -first_sin], axis=0), stacked)
    twiddle = angles_of(
        jnp.arange(kept, dtype=jnp.int32)[:, None]
        * jnp.arange(row_count, dtype=jnp.int32)[None, :],
        padded,
    )[:, None, :]
    real_part = first[:kept]
    imag_part = first[kept:]
    cosine = jnp.cos(twiddle)
    sine_part = jnp.sin(twiddle)
    rotated = jnp.concatenate([real_part, imag_part], axis=2) * jnp.concatenate(
        [cosine, cosine], axis=2
    ) + jnp.concatenate([imag_part, real_part], axis=2) * jnp.concatenate(
        [sine_part, -sine_part], axis=2
    )
    second_cos, second_sin = dft_table(row_count, row_count, row_count)
    prod = contract("kcb,bq->kcq", rotated, complex_table(second_cos, second_sin, -1))
    data_real = prod[:, :own_width, :row_count]
    data_imag = prod[:, :own_width, row_count:]
    filter_real = prod[:, own_width:, :row_count]
    filter_imag = prod[:, own_width:, row_count:]
    spec_real = data_real * filter_real - data_imag * filter_imag
    spec_imag = data_real * filter_imag + data_imag * filter_real
    prod = contract(
        "kcq,qb->kcb",
        jnp.concatenate([spec_real, spec_imag], axis=2),
        complex_table(second_cos, second_sin, 1),
    )
    real_part, imag_part = rotate(prod[:, :, :row_count], prod[:, :, row_count:], twiddle, 1)
    back_cos, back_sin = dft_table(n_dev, kept, size_a)
    index = jnp.arange(kept)
    weight = jnp.where((index == 0) | (index == n_dev), 1.0, 2.0).astype(jnp.float32)[None, :]
    outcome = contract(
        "nk,kcb->ncb",
        jnp.concatenate([back_cos * weight, -back_sin * weight], axis=1),
        jnp.concatenate([real_part, imag_part], axis=0),
    )
    return (outcome * (1.0 / padded)).astype(jnp.bfloat16)


def by_channels(mixed, key_in, value_in, filters, group_index):
    n_dev = lax.axis_size("outer") * lax.axis_size("inner")
    row_count = mixed.shape[0]
    channels = mixed.shape[1]
    own_width = channels // n_dev
    pieces = 1
    piece_width = own_width // pieces
    if piece_width % 16 == 0:
        sent = prepare(key_in, value_in, filters, group_index, n_dev, pieces)
    else:
        chan_filters = select_filters(filters, group_index)
        sent = jnp.stack([mixed.T, chan_filters], axis=0).reshape(
            2, n_dev, pieces, piece_width, row_count
        )
        sent = sent.transpose(2, 1, 0, 3, 4)
    arrived = [
        lax.all_to_all(sent[piece], ("outer", "inner"), split_axis=0, concat_axis=0, tiled=True)
        for piece in range(pieces)
    ]
    results = []
    outcome = None
    for piece in range(pieces):
        got = arrived[piece]
        if outcome is not None:
            outcome, got = lax.optimization_barrier((outcome, got))
        outcome = convolve_block(got, n_dev, row_count)
        results.append(outcome)
    returned = lax.all_to_all(
        jnp.stack(results, axis=1), ("outer", "inner"), split_axis=0, concat_axis=0, tiled=True
    )
    return returned.reshape(channels, row_count)


def on_device(query, key_in, value_in, filters, group_index, skip_gain):
    mixed = (key_in.astype(jnp.float32) * value_in.astype(jnp.float32)).astype(jnp.bfloat16)
    convolved = by_channels(mixed, key_in, value_in, filters, group_index).T.astype(jnp.float32)
    mixed_wide = mixed.astype(jnp.float32)
    return (query.astype(jnp.float32) * (convolved + skip_gain[None, :] * mixed_wide)).astype(
        jnp.bfloat16
    )


def solution(mesh):
    placed = (
        P(("outer", "inner"), None),
        P(("outer", "inner"), None),
        P(("outer", "inner"), None),
        P(("outer", "inner"), None),
        P(),
        P(),
    )
    return jax.shard_map(
        on_device,
        mesh=mesh,
        in_specs=placed,
        out_specs=P(("outer", "inner"), None),
        check_vma=False,
    )
```

```python
import math

import jax
import jax.numpy as jnp
from jax import lax
from jax.sharding import PartitionSpec as P
from jax.experimental import pallas as pl


def contract(pattern, left_op, right_op):
    return jnp.einsum(
        pattern,
        left_op,
        right_op,
        precision=lax.Precision.HIGH,
        preferred_element_type=jnp.float32,
    )


def angles_of(numerator, period):
    return 2.0 * math.pi / period * jnp.mod(numerator, period).astype(jnp.float32)


def dft_table(count_out, count_in, period):
    index_grid = (
        jnp.arange(count_out, dtype=jnp.int32)[:, None]
        * jnp.arange(count_in, dtype=jnp.int32)[None, :]
    )
    phases = angles_of(index_grid, period)
    return (jnp.cos(phases), jnp.sin(phases))


def rotate(real_part, imag_part, phases, direction):
    cosine = jnp.cos(phases)
    sine_part = jnp.sin(phases)
    if direction < 0:
        return (
            real_part * cosine + imag_part * sine_part,
            imag_part * cosine - real_part * sine_part,
        )
    return (real_part * cosine - imag_part * sine_part, imag_part * cosine + real_part * sine_part)


def transform(pattern, table_cos, table_sin, real_part, imag_part, direction):
    out_real = contract(pattern, table_cos, real_part) - direction * contract(
        pattern, table_sin, imag_part
    )
    out_imag = contract(pattern, table_cos, imag_part) + direction * contract(
        pattern, table_sin, real_part
    )
    return (out_real, out_imag)


def select_kernel(index_ref, filters_ref, out_ref):
    index = index_ref[...]
    groups = filters_ref.shape[1]
    onehot = (
        index == lax.broadcasted_iota(jnp.int32, (index.shape[0], groups), 1)
    ).astype(jnp.bfloat16)
    out_ref[...] = lax.dot_general(
        onehot,
        filters_ref[...],
        (((1,), (1,)), ((), ())),
        preferred_element_type=jnp.float32,
    ).astype(out_ref.dtype)


def select_filters(filters, group_index):
    channels = group_index.shape[0]
    return pl.pallas_call(
        select_kernel,
        out_shape=jax.ShapeDtypeStruct((channels, filters.shape[0]), jnp.bfloat16),
    )(group_index.reshape(channels, 1), filters)


def prep_kernel(key_ref, value_ref, filters_ref, index_ref, *out_refs):
    pieces = len(out_refs)
    n_dev, _, piece_width, _ = out_refs[0].shape
    mixed = (key_ref[...].astype(jnp.float32) * value_ref[...].astype(jnp.float32)).astype(
        jnp.bfloat16
    )
    mixed_t = mixed.astype(jnp.float32).T
    groups = filters_ref.shape[1]
    channels = index_ref.shape[1]
    onehot_t = (
        lax.broadcasted_iota(jnp.int32, (groups, channels), 0) == index_ref[...]
    ).astype(jnp.bfloat16)
    picked = jnp.dot(filters_ref[...], onehot_t, preferred_element_type=jnp.float32).T
    for dest in range(n_dev):
        for piece in range(pieces):
            low = (dest * pieces + piece) * piece_width
            out_refs[piece][dest, 0] = mixed_t[low : low + piece_width].astype(jnp.bfloat16)
            out_refs[piece][dest, 1] = picked[low : low + piece_width].astype(jnp.bfloat16)


def prepare(key_in, value_in, filters, group_index, n_dev, pieces):
    row_count, channels = key_in.shape
    piece_width = channels // (n_dev * pieces)
    return pl.pallas_call(
        prep_kernel,
        out_shape=tuple(
            jax.ShapeDtypeStruct((n_dev, 2, piece_width, row_count), jnp.bfloat16)
            for _ in range(pieces)
        ),
    )(key_in, value_in, filters, group_index.reshape(1, channels))


def finish_kernel(returned_ref, query_ref, key_ref, value_ref, gain_ref, out_ref):
    convolved = returned_ref[...].astype(jnp.float32).T
    mixed = (key_ref[...].astype(jnp.float32) * value_ref[...].astype(jnp.float32)).astype(
        jnp.bfloat16
    )
    out_ref[...] = (
        query_ref[...].astype(jnp.float32)
        * (convolved + gain_ref[...] * mixed.astype(jnp.float32))
    ).astype(out_ref.dtype)


def finish(returned, query, key_in, value_in, skip_gain):
    return pl.pallas_call(
        finish_kernel,
        out_shape=jax.ShapeDtypeStruct(query.shape, jnp.bfloat16),
    )(returned, query, key_in, value_in, skip_gain.reshape(1, -1))


def complex_table(cos_part, sin_part, direction):
    return jnp.concatenate(
        [
            jnp.concatenate([cos_part, direction * sin_part], axis=1),
            jnp.concatenate([-direction * sin_part, cos_part], axis=1),
        ],
        axis=0,
    )


def convolve_block(got, n_dev, row_count):
    own_width = got.shape[2]
    size_a = 2 * n_dev
    kept = n_dev + 1
    padded = size_a * row_count
    stacked = got.reshape(n_dev, 2 * own_width, row_count).astype(jnp.float32)
    first_cos, first_sin = dft_table(kept, n_dev, size_a)
    first = contract("kn,ncb->kcb", jnp.concatenate([first_cos, -first_sin], axis=0), stacked)
    twiddle = angles_of(
        jnp.arange(kept, dtype=jnp.int32)[:, None]
        * jnp.arange(row_count, dtype=jnp.int32)[None, :],
        padded,
    )[:, None, :]
    real_part, imag_part = rotate(first[:kept], first[kept:], twiddle, -1)
    second_cos, second_sin = dft_table(row_count, row_count, row_count)
    prod = contract(
        "kcb,bq->kcq",
        jnp.concatenate([real_part, imag_part], axis=2),
        complex_table(second_cos, second_sin, -1),
    )
    data_real = prod[:, :own_width, :row_count]
    data_imag = prod[:, :own_width, row_count:]
    filter_real = prod[:, own_width:, :row_count]
    filter_imag = prod[:, own_width:, row_count:]
    spec_real = data_real * filter_real - data_imag * filter_imag
    spec_imag = data_real * filter_imag + data_imag * filter_real
    prod = contract(
        "kcq,qb->kcb",
        jnp.concatenate([spec_real, spec_imag], axis=2),
        complex_table(second_cos, second_sin, 1),
    )
    real_part = prod[:, :, :row_count]
    imag_part = prod[:, :, row_count:]
    cosine = jnp.cos(twiddle)
    sine_part = jnp.sin(twiddle)
    stacked_back = jnp.concatenate([real_part, imag_part], axis=0) * jnp.concatenate(
        [cosine, cosine], axis=0
    ) + jnp.concatenate([imag_part, real_part], axis=0) * jnp.concatenate(
        [-sine_part, sine_part], axis=0
    )
    back_cos, back_sin = dft_table(n_dev, kept, size_a)
    index = jnp.arange(kept)
    weight = jnp.where((index == 0) | (index == n_dev), 1.0, 2.0).astype(jnp.float32)[None, :]
    outcome = contract(
        "nk,kcb->ncb",
        jnp.concatenate([back_cos * weight, -back_sin * weight], axis=1),
        stacked_back,
    )
    return (outcome * (1.0 / padded)).astype(jnp.bfloat16)


def by_channels(mixed, key_in, value_in, filters, group_index):
    n_dev = lax.axis_size("outer") * lax.axis_size("inner")
    row_count = mixed.shape[0]
    channels = mixed.shape[1]
    own_width = channels // n_dev
    pieces = 1
    piece_width = own_width // pieces
    if piece_width % 16 == 0:
        sent = prepare(key_in, value_in, filters, group_index, n_dev, pieces)
    else:
        chan_filters = select_filters(filters, group_index)
        sent = jnp.stack([mixed.T, chan_filters], axis=0).reshape(
            2, n_dev, pieces, piece_width, row_count
        )
        sent = sent.transpose(2, 1, 0, 3, 4)
    arrived = [
        lax.all_to_all(sent[piece], ("outer", "inner"), split_axis=0, concat_axis=0, tiled=True)
        for piece in range(pieces)
    ]
    results = []
    outcome = None
    for piece in range(pieces):
        got = arrived[piece]
        if outcome is not None:
            outcome, got = lax.optimization_barrier((outcome, got))
        outcome = convolve_block(got, n_dev, row_count)
        results.append(outcome)
    returned = lax.all_to_all(
        jnp.stack(results, axis=1), ("outer", "inner"), split_axis=0, concat_axis=0, tiled=True
    )
    return returned.reshape(channels, row_count)


def on_device(query, key_in, value_in, filters, group_index, skip_gain):
    mixed = (key_in.astype(jnp.float32) * value_in.astype(jnp.float32)).astype(jnp.bfloat16)
    convolved = by_channels(mixed, key_in, value_in, filters, group_index).T.astype(jnp.float32)
    mixed_wide = mixed.astype(jnp.float32)
    return (query.astype(jnp.float32) * (convolved + skip_gain[None, :] * mixed_wide)).astype(
        jnp.bfloat16
    )


def solution(mesh):
    placed = (
        P(("outer", "inner"), None),
        P(("outer", "inner"), None),
        P(("outer", "inner"), None),
        P(("outer", "inner"), None),
        P(),
        P(),
    )
    return jax.shard_map(
        on_device,
        mesh=mesh,
        in_specs=placed,
        out_specs=P(("outer", "inner"), None),
        check_vma=False,
    )
```

```python
import math

import jax
import jax.numpy as jnp
from jax import lax
from jax.sharding import PartitionSpec as P
from jax.experimental import pallas as pl


def contract(pattern, left_op, right_op):
    return jnp.einsum(
        pattern,
        left_op,
        right_op,
        precision=lax.Precision.HIGH,
        preferred_element_type=jnp.float32,
    )


def angles_of(numerator, period):
    return 2.0 * math.pi / period * jnp.mod(numerator, period).astype(jnp.float32)


def dft_table(count_out, count_in, period):
    index_grid = (
        jnp.arange(count_out, dtype=jnp.int32)[:, None]
        * jnp.arange(count_in, dtype=jnp.int32)[None, :]
    )
    phases = angles_of(index_grid, period)
    return (jnp.cos(phases), jnp.sin(phases))


def rotate(real_part, imag_part, phases, direction):
    cosine = jnp.cos(phases)
    sine_part = jnp.sin(phases)
    if direction < 0:
        return (
            real_part * cosine + imag_part * sine_part,
            imag_part * cosine - real_part * sine_part,
        )
    return (real_part * cosine - imag_part * sine_part, imag_part * cosine + real_part * sine_part)


def transform(pattern, table_cos, table_sin, real_part, imag_part, direction):
    out_real = contract(pattern, table_cos, real_part) - direction * contract(
        pattern, table_sin, imag_part
    )
    out_imag = contract(pattern, table_cos, imag_part) + direction * contract(
        pattern, table_sin, real_part
    )
    return (out_real, out_imag)


def select_kernel(index_ref, filters_ref, out_ref):
    index = index_ref[...]
    groups = filters_ref.shape[1]
    onehot = (
        index == lax.broadcasted_iota(jnp.int32, (index.shape[0], groups), 1)
    ).astype(jnp.bfloat16)
    out_ref[...] = lax.dot_general(
        onehot,
        filters_ref[...],
        (((1,), (1,)), ((), ())),
        preferred_element_type=jnp.float32,
    ).astype(out_ref.dtype)


def select_filters(filters, group_index):
    channels = group_index.shape[0]
    return pl.pallas_call(
        select_kernel,
        out_shape=jax.ShapeDtypeStruct((channels, filters.shape[0]), jnp.bfloat16),
    )(group_index.reshape(channels, 1), filters)


def prep_kernel(key_ref, value_ref, filters_ref, index_ref, *out_refs):
    pieces = len(out_refs)
    n_dev, _, piece_width, _ = out_refs[0].shape
    mixed = (key_ref[...].astype(jnp.float32) * value_ref[...].astype(jnp.float32)).astype(
        jnp.bfloat16
    )
    mixed_t = mixed.astype(jnp.float32).T
    groups = filters_ref.shape[1]
    channels = index_ref.shape[1]
    onehot_t = (
        lax.broadcasted_iota(jnp.int32, (groups, channels), 0) == index_ref[...]
    ).astype(jnp.bfloat16)
    picked = jnp.dot(filters_ref[...], onehot_t, preferred_element_type=jnp.float32).T
    for dest in range(n_dev):
        for piece in range(pieces):
            low = (dest * pieces + piece) * piece_width
            out_refs[piece][dest, 0] = mixed_t[low : low + piece_width].astype(jnp.bfloat16)
            out_refs[piece][dest, 1] = picked[low : low + piece_width].astype(jnp.bfloat16)


def prepare(key_in, value_in, filters, group_index, n_dev, pieces):
    row_count, channels = key_in.shape
    piece_width = channels // (n_dev * pieces)
    return pl.pallas_call(
        prep_kernel,
        out_shape=tuple(
            jax.ShapeDtypeStruct((n_dev, 2, piece_width, row_count), jnp.bfloat16)
            for _ in range(pieces)
        ),
    )(key_in, value_in, filters, group_index.reshape(1, channels))


def finish_kernel(returned_ref, query_ref, key_ref, value_ref, gain_ref, out_ref):
    convolved = returned_ref[...].astype(jnp.float32).T
    mixed = (key_ref[...].astype(jnp.float32) * value_ref[...].astype(jnp.float32)).astype(
        jnp.bfloat16
    )
    out_ref[...] = (
        query_ref[...].astype(jnp.float32)
        * (convolved + gain_ref[...] * mixed.astype(jnp.float32))
    ).astype(out_ref.dtype)


def finish(returned, query, key_in, value_in, skip_gain):
    return pl.pallas_call(
        finish_kernel,
        out_shape=jax.ShapeDtypeStruct(query.shape, jnp.bfloat16),
    )(returned, query, key_in, value_in, skip_gain.reshape(1, -1))


def complex_table(cos_part, sin_part, direction):
    return jnp.concatenate(
        [
            jnp.concatenate([cos_part, direction * sin_part], axis=1),
            jnp.concatenate([-direction * sin_part, cos_part], axis=1),
        ],
        axis=0,
    )


def convolve_block(got, n_dev, row_count):
    own_width = got.shape[2]
    size_a = 2 * n_dev
    kept = n_dev + 1
    padded = size_a * row_count
    stacked = got.reshape(n_dev, 2 * own_width, row_count).astype(jnp.float32)
    first_cos, first_sin = dft_table(kept, n_dev, size_a)
    first = contract("kn,ncb->kcb", jnp.concatenate([first_cos, -first_sin], axis=0), stacked)
    twiddle = angles_of(
        jnp.arange(kept, dtype=jnp.int32)[:, None]
        * jnp.arange(row_count, dtype=jnp.int32)[None, :],
        padded,
    )[:, None, :]
    real_part, imag_part = rotate(first[:kept], first[kept:], twiddle, -1)
    second_cos, second_sin = dft_table(row_count, row_count, row_count)
    prod = contract(
        "kcb,bq->kcq",
        jnp.concatenate([real_part, imag_part], axis=2),
        complex_table(second_cos, second_sin, -1),
    )
    data_real = prod[:, :own_width, :row_count]
    data_imag = prod[:, :own_width, row_count:]
    filter_real = prod[:, own_width:, :row_count]
    filter_imag = prod[:, own_width:, row_count:]
    spec_real = data_real * filter_real - data_imag * filter_imag
    spec_imag = data_real * filter_imag + data_imag * filter_real
    prod = contract(
        "kcq,qb->kcb",
        jnp.concatenate([spec_real, spec_imag], axis=2),
        complex_table(second_cos, second_sin, 1),
    )
    real_part, imag_part = rotate(prod[:, :, :row_count], prod[:, :, row_count:], twiddle, 1)
    back_cos, back_sin = dft_table(n_dev, kept, size_a)
    index = jnp.arange(kept)
    weight = jnp.where((index == 0) | (index == n_dev), 1.0, 2.0).astype(jnp.float32)[None, :]
    outcome = contract(
        "nk,kcb->ncb",
        jnp.concatenate([back_cos * weight, -back_sin * weight], axis=1) * (1.0 / padded),
        jnp.concatenate([real_part, imag_part], axis=0),
    )
    return outcome.astype(jnp.bfloat16)


def by_channels(mixed, key_in, value_in, filters, group_index):
    n_dev = lax.axis_size("outer") * lax.axis_size("inner")
    row_count = mixed.shape[0]
    channels = mixed.shape[1]
    own_width = channels // n_dev
    pieces = 1
    piece_width = own_width // pieces
    if piece_width % 16 == 0:
        sent = prepare(key_in, value_in, filters, group_index, n_dev, pieces)
    else:
        chan_filters = select_filters(filters, group_index)
        sent = jnp.stack([mixed.T, chan_filters], axis=0).reshape(
            2, n_dev, pieces, piece_width, row_count
        )
        sent = sent.transpose(2, 1, 0, 3, 4)
    arrived = [
        lax.all_to_all(sent[piece], ("outer", "inner"), split_axis=0, concat_axis=0, tiled=True)
        for piece in range(pieces)
    ]
    results = []
    outcome = None
    for piece in range(pieces):
        got = arrived[piece]
        if outcome is not None:
            outcome, got = lax.optimization_barrier((outcome, got))
        outcome = convolve_block(got, n_dev, row_count)
        results.append(outcome)
    returned = lax.all_to_all(
        jnp.stack(results, axis=1), ("outer", "inner"), split_axis=0, concat_axis=0, tiled=True
    )
    return returned.reshape(channels, row_count)


def on_device(query, key_in, value_in, filters, group_index, skip_gain):
    mixed = (key_in.astype(jnp.float32) * value_in.astype(jnp.float32)).astype(jnp.bfloat16)
    convolved = by_channels(mixed, key_in, value_in, filters, group_index).T.astype(jnp.float32)
    mixed_wide = mixed.astype(jnp.float32)
    return (query.astype(jnp.float32) * (convolved + skip_gain[None, :] * mixed_wide)).astype(
        jnp.bfloat16
    )


def solution(mesh):
    placed = (
        P(("outer", "inner"), None),
        P(("outer", "inner"), None),
        P(("outer", "inner"), None),
        P(("outer", "inner"), None),
        P(),
        P(),
    )
    return jax.shard_map(
        on_device,
        mesh=mesh,
        in_specs=placed,
        out_specs=P(("outer", "inner"), None),
        check_vma=False,
    )
```
